32 devices in a mesh: cuts: 8 (over y, x, core), row: 4 (over z).
Axes of the slice: x: 2, y: 2, z: 4, core: 2. Of those that a mesh axis runs over, the one named last changes fastest.
Arguments:
- vectors: bfloat16 [8, 128, 98304], P('cuts', None, 'row'), may hold values from -100 to 100
- counts: int32 [8], P('cuts'), may hold values from 64 to 128, as said below
- offsets: int32 [8, 2], P('cuts'), may hold values from 0 to 96, as said below
- margin_blocks: bfloat16 [1024, 96, 288], P('row'), may hold values from -0.5 to 1.5
- energy_blocks: bfloat16 [1024, 96, 288], P('row'), may hold values from -1 to 6
- block_columns: int32 [1024, 3], P('row'), may hold values from 0 to 1023, as said below
Outputs:
- ritz_residual: bfloat16 [8, 128, 98304], P('cuts', None, 'row')
- margin_pencil: float32 [8, 128, 128], P('cuts')
- energy_pencil: float32 [8, 128, 128], P('cuts')
The draws below stay inside these ranges and needn't reach their ends.
Inputs may be any that keep to these rules, and one draw needn't show every extreme that they name: `counts`: some slice has all 128 vectors valid and another exactly 64. offsets[s, 0] is at most 8; offsets[s, 1] + 32 lies between counts[s] - 8 and counts[s]; so both windows lie among the valid vectors. block_columns[i, 0] = i, block_columns[i, 1] lies in i - 2 to i and block_columns[i, 2] in i to i + 2.
All inputs are finite; a program needn't handle non-finite values.
Results may differ from the reference program's by a relative error of at most 0.00225.
The reference program's roundings to bfloat16 on the way count: a program that leaves them out, or rounds other values in their place, can miss the bound.
Values may be sent and summed in bfloat16 or wider, within the bound.
No kernel may reach another device: no remote copies, remote signals or barrier semaphores. Data moves between devices by JAX's collectives and lax.ppermute only.
A program may use at most 256 MiB of HBM per device.

```python
import math
import jax
import jax.numpy as jnp
from jax import lax

BLK = 96
NNZ = 3
NMAT = 98304
KV = 128
WIN = 32
NSLICE = 8
NB = 1024
NB_DEV = 256


def slice_meta(key):
    meta_key = jax.random.fold_in(key, 11)
    keys = jax.random.split(meta_key, 5)
    positions = jnp.arange(NSLICE, dtype=jnp.int32)
    counts_raw = jax.random.randint(keys[0], (NSLICE,), KV // 2, KV + 1)
    full_slice = jax.random.randint(keys[1], (), 0, NSLICE)
    short_slice = (full_slice + 1 + jax.random.randint(keys[2], (), 0, NSLICE - 1)) % NSLICE
    counts_all = jnp.where(positions == full_slice, KV, jnp.where(positions == short_slice, KV // 2, counts_raw))
    slack_count = WIN // 4
    lower_start = jax.random.randint(keys[3], (NSLICE,), 0, slack_count + 1)
    upper_gap = jax.random.randint(keys[4], (NSLICE,), 0, slack_count + 1)
    lower_start = jnp.where(positions == full_slice, 0, lower_start)
    upper_gap = jnp.where(positions == full_slice, 0, upper_gap)
    starts = jnp.stack([lower_start, counts_all - WIN - upper_gap], axis=1)
    return (counts_all.astype(jnp.int32), starts.astype(jnp.int32))


def draw_counts(key, part):
    return slice_meta(key)[0]


def draw_offsets(key, part):
    return slice_meta(key)[1]


def draw_vectors(key, part):
    counts_all, starts = slice_meta(key)
    rough_rows = jax.random.uniform(jax.random.fold_in(key, 29), (NMAT,), jnp.float32)
    trend_rows = jnp.arange(NMAT, dtype=jnp.float32) / NMAT
    row_scale = 10.0 ** (rough_rows - 0.5) * 3.0 ** (0.5 * (trend_rows - 0.5))
    noise_key = jax.random.fold_in(key, 31)
    pick_key = jax.random.fold_in(key, 37)
    column_key = jax.random.fold_in(key, 41)

    def raw_vectors(index):
        inside = ((index >= 0) & (index < NSLICE)).astype(jnp.float32)
        safe_index = jnp.clip(index, 0, NSLICE - 1)
        own_key = jax.random.fold_in(noise_key, safe_index)
        noise = jnp.clip(jax.random.normal(own_key, (KV, NMAT), jnp.float32), -4.0, 4.0)
        column_scale = 10.0 ** (jax.random.uniform(jax.random.fold_in(column_key, safe_index), (KV,), jnp.float32) - 0.5)
        return noise * column_scale[:, None] * row_scale[None, :] * inside

    def one_slice(index):
        total = raw_vectors(index)
        pick_keys = jax.random.split(jax.random.fold_in(pick_key, index), 2)
        side_pick = jax.random.randint(pick_keys[0], (KV,), 0, 4)
        within = jax.random.randint(pick_keys[1], (KV,), 0, WIN)
        for side_index, pairing in enumerate(((-2, 1), (-1, 1), (1, 0), (2, 0))):
            neighbour = index + pairing[0]
            start = starts[jnp.clip(neighbour, 0, NSLICE - 1), pairing[1]]
            source = jnp.take(raw_vectors(neighbour), start + within, axis=0)
            total = total + 0.8 * jnp.where((side_pick == side_index)[:, None], source, jnp.float32(0.0))
        return total.astype(jnp.bfloat16)
    return lax.map(one_slice, jnp.arange(NSLICE, dtype=jnp.int32))


def block_noise(key):
    shape = (NB, BLK, NNZ * BLK)
    coupling = jnp.clip(jax.random.normal(key, shape, jnp.float32), -4.0, 4.0)
    return coupling / math.sqrt(NNZ * BLK)


def block_identity():
    out_index = jnp.arange(BLK, dtype=jnp.int32)[:, None]
    in_index = jnp.arange(NNZ * BLK, dtype=jnp.int32)[None, :]
    return (out_index == in_index).astype(jnp.float32)


def draw_margin_blocks(key, part):
    coupling = block_noise(jax.random.fold_in(key, 53))
    return (block_identity()[None] + 0.6 * coupling).astype(jnp.bfloat16)


def draw_energy_blocks(key, part):
    coupling = block_noise(jax.random.fold_in(key, 59))
    energies = 0.5 + 4.5 * jax.random.uniform(jax.random.fold_in(key, 61), (NB, BLK), jnp.float32)
    return (block_identity()[None] * energies[:, :, None] + coupling).astype(jnp.bfloat16)


def draw_block_columns(key, part):
    keys = jax.random.split(jax.random.fold_in(key, 67), 2)
    block_index = jnp.arange(NB, dtype=jnp.int32)
    within_dev = block_index % NB_DEV
    below = jax.random.randint(keys[0], (NB,), 1, 3)
    above = jax.random.randint(keys[1], (NB,), 1, 3)
    below = jnp.where(within_dev == 1, 2, below)
    above = jnp.where(within_dev == NB_DEV - 2, 2, above)
    first_col = block_index
    second_col = jnp.clip(block_index - below, 0, NB - 1)
    third_col = jnp.clip(block_index + above, 0, NB - 1)
    return jnp.stack([first_col, second_col, third_col], axis=1).astype(jnp.int32)


def setup_inputs(seed: int = 0) -> dict:
    arg_keys = jax.random.split(jax.random.key(seed), 7)
    vectors = draw_vectors(jax.random.fold_in(arg_keys[6], 71), 0)
    counts = draw_counts(jax.random.fold_in(arg_keys[6], 71), 0)
    offsets = draw_offsets(jax.random.fold_in(arg_keys[6], 71), 0)
    margin_blocks = draw_margin_blocks(jax.random.fold_in(arg_keys[6], 71), 0)
    energy_blocks = draw_energy_blocks(jax.random.fold_in(arg_keys[6], 71), 0)
    block_columns = draw_block_columns(jax.random.fold_in(arg_keys[6], 71), 0)
    return {"vectors": vectors, "counts": counts, "offsets": offsets, "margin_blocks": margin_blocks, "energy_blocks": energy_blocks, "block_columns": block_columns}


def apply_blocks(matrices, block_columns, field):
    width = field.shape[0]
    grid = field.astype(jnp.float32).reshape(width, NB, BLK)
    picked = jnp.take(grid, block_columns.reshape(-1), axis=1).reshape(width, NB, NNZ, BLK)
    return jnp.einsum('cnkb,nakb->cna', picked, matrices).reshape(width, NMAT)


def take_window(rows_of, start):
    return lax.dynamic_slice_in_dim(rows_of, start.astype(jnp.int32), WIN, 0)


def reference(vectors, counts, offsets, margin_blocks, energy_blocks, block_columns):
    positions = jnp.arange(KV, dtype=jnp.int32)
    lower_all = jax.vmap(take_window)(vectors, offsets[:, 0])
    upper_all = jax.vmap(take_window)(vectors, offsets[:, 1])
    zero_pad = ((2, 2), (0, 0), (0, 0))
    lower_pad = jnp.pad(lower_all, zero_pad)
    upper_pad = jnp.pad(upper_all, zero_pad)
    margin_mats = margin_blocks.astype(jnp.float32).reshape(NB, BLK, NNZ, BLK)
    energy_mats = energy_blocks.astype(jnp.float32).reshape(NB, BLK, NNZ, BLK)

    def one_slice(index):
        valid_mask = positions < counts[index]
        masked = jnp.where(valid_mask[:, None], vectors[index], jnp.zeros((), vectors.dtype))
        windows = jnp.concatenate([upper_pad[index], upper_pad[index + 1], lower_pad[index + 3], lower_pad[index + 4]], axis=0)
        margin_windows = apply_blocks(margin_mats, block_columns, windows).astype(jnp.bfloat16)
        margin = jnp.dot(margin_windows, masked.T, preferred_element_type=jnp.float32) / NMAT
        removed = jnp.dot(margin.astype(jnp.bfloat16).T, windows, preferred_element_type=jnp.float32)
        cleaned = (masked.astype(jnp.float32) - removed).astype(jnp.bfloat16)
        margin_cleaned = apply_blocks(margin_mats, block_columns, cleaned).astype(jnp.bfloat16)
        energy_cleaned = apply_blocks(energy_mats, block_columns, cleaned).astype(jnp.bfloat16)
        margin_pencil = jnp.dot(cleaned, margin_cleaned.T, preferred_element_type=jnp.float32) / NMAT
        energy_pencil = jnp.dot(cleaned, energy_cleaned.T, preferred_element_type=jnp.float32) / NMAT
        margin_diag = jnp.diagonal(margin_pencil)
        energy_diag = jnp.diagonal(energy_pencil)
        theta = jnp.where(valid_mask, energy_diag / jnp.where(valid_mask, margin_diag, jnp.float32(1.0)), jnp.float32(0.0))
        residual = (energy_cleaned.astype(jnp.float32) - theta[:, None] * margin_cleaned.astype(jnp.float32)).astype(jnp.bfloat16)
        return residual, margin_pencil, energy_pencil

    ritz_residual, margin_pencil, energy_pencil = lax.map(one_slice, jnp.arange(NSLICE, dtype=jnp.int32))
    return (ritz_residual, margin_pencil, energy_pencil)
```

```python
import functools

import jax
import jax.numpy as jnp
from jax import lax
from jax.experimental import pallas as pl
from jax.experimental.pallas import tpu as pltpu
from jax.sharding import PartitionSpec as P

WIN = 32
NNZ = 3
HALO = 2


def from_behind(block, axis, distance):
    devices = range(lax.axis_size(axis))
    route = [(i - distance, i) for i in devices if i - distance in devices]
    return lax.ppermute(block, axis, route)


def row_halos(cells, width):
    count = lax.axis_size("row")
    ends = count - 1
    head = cells[:width]
    tail = cells[cells.shape[0] - width :]
    lower = lax.ppermute(tail, "row", [(i, i + 1) for i in range(ends)])
    upper = lax.ppermute(head, "row", [(i + 1, i) for i in range(ends)])
    return lower, upper


def apply_kernel(shift_ref, x_hbm, lo_ref, hi_ref, *refs, group, blk, nmat):
    mats = refs[:nmat]
    outs = refs[nmat : 2 * nmat]
    xpad, sem = refs[2 * nmat], refs[2 * nmat + 1]
    g = pl.program_id(0)
    entries = x_hbm.shape[0]
    halo = HALO * blk

    @pl.when(g == 0)
    def _():
        copy = pltpu.make_async_copy(x_hbm, xpad.at[pl.ds(halo, entries)], sem.at[0])
        copy.start()
        xpad[pl.ds(0, halo), :] = lo_ref[...]
        xpad[pl.ds(halo + entries, halo), :] = hi_ref[...]
        copy.wait()

    def body(j, carry):
        row = g * group + j
        parts = []
        for k in range(NNZ):
            src = row + shift_ref[row * NNZ + k] + HALO
            start = pl.multiple_of(src * blk, 16)
            parts.append(xpad[pl.ds(start, blk), :])
        xs = jnp.concatenate(parts, axis=0)
        for m in range(nmat):
            r = jnp.dot(mats[m][j], xs, preferred_element_type=jnp.float32)
            outs[m][pl.ds(pl.multiple_of(j * blk, 16), blk), :] = r.astype(outs[m].dtype)
        return carry

    lax.fori_loop(0, group, body, 0)


def block_apply(matrices, shifts_flat, cells):
    entries, slots = cells.shape
    block_rows, blk, width = matrices[0].shape
    lower, upper = row_halos(cells, HALO * blk)
    group = 32 if block_rows % 32 == 0 else block_rows
    nmat = len(matrices)
    kernel = functools.partial(apply_kernel, group=group, blk=blk, nmat=nmat)
    mat_spec = pl.BlockSpec((group, blk, width), lambda g, s: (g, 0, 0))
    out_spec = pl.BlockSpec((group * blk, slots), lambda g, s: (g, 0))
    halo_spec = pl.BlockSpec((HALO * blk, slots), lambda g, s: (0, 0))
    grid_spec = pltpu.PrefetchScalarGridSpec(
        num_scalar_prefetch=1,
        grid=(block_rows // group,),
        in_specs=[pl.BlockSpec(memory_space=pl.ANY), halo_spec, halo_spec] + [mat_spec] * nmat,
        out_specs=[out_spec] * nmat,
        scratch_shapes=[
            pltpu.VMEM((entries + 2 * HALO * blk, slots), cells.dtype),
            pltpu.SemaphoreType.DMA((1,)),
        ],
    )
    return pl.pallas_call(
        kernel,
        grid_spec=grid_spec,
        out_shape=[jax.ShapeDtypeStruct((entries, slots), jnp.bfloat16)] * nmat,
        compiler_params=pltpu.CompilerParams(dimension_semantics=("arbitrary",)),
    )(shifts_flat, cells, lower, upper, *matrices)


def tn_dot(a, b):
    return lax.dot_general(a, b, (((0,), (0,)), ((), ())), preferred_element_type=jnp.float32)


def shards(vectors, counts, offsets, margin_blocks, energy_blocks, block_columns):
    own_vectors = vectors[0]
    vector_count, entries = own_vectors.shape
    nmat_total = entries * lax.axis_size("row")
    block_rows = margin_blocks.shape[0]
    valid_mask = jnp.arange(vector_count, dtype=jnp.int32) < counts[0]
    masked = jnp.where(valid_mask[:, None], own_vectors, jnp.zeros((), own_vectors.dtype))
    lower_window = lax.dynamic_slice_in_dim(masked, offsets[0, 0], WIN, 0)
    upper_window = lax.dynamic_slice_in_dim(masked, offsets[0, 1], WIN, 0)
    own_blocks = lax.axis_index("row") * block_rows + jnp.arange(block_rows, dtype=jnp.int32)
    shifts_flat = (block_columns - own_blocks[:, None]).reshape(-1)
    from_below = [from_behind(upper_window, "cuts", distance) for distance in (2, 1)]
    from_above = [from_behind(lower_window, "cuts", -distance) for distance in (1, 2)]
    masked_t = masked.T
    windows_t = jnp.concatenate(from_below + from_above, axis=0).T
    (margin_windows_t,) = block_apply((margin_blocks,), shifts_flat, windows_t)
    partial_margin = tn_dot(margin_windows_t, masked_t)
    margin = lax.psum(partial_margin, "row") / nmat_total
    removed_t = jnp.dot(windows_t, margin.astype(jnp.bfloat16), preferred_element_type=jnp.float32)
    cleaned_t = (masked_t.astype(jnp.float32) - removed_t).astype(jnp.bfloat16)
    margin_cleaned_t, energy_cleaned_t = block_apply(
        (margin_blocks, energy_blocks), shifts_flat, cleaned_t
    )
    margin_part = tn_dot(cleaned_t, margin_cleaned_t)
    energy_part = tn_dot(cleaned_t, energy_cleaned_t)
    margin_total, energy_total = lax.psum((margin_part, energy_part), "row")
    margin_pencil = margin_total / nmat_total
    energy_pencil = energy_total / nmat_total
    margin_diag = jnp.diagonal(margin_pencil)
    energy_diag = jnp.diagonal(energy_pencil)
    theta = jnp.where(
        valid_mask,
        energy_diag / jnp.where(valid_mask, margin_diag, jnp.float32(1.0)),
        jnp.float32(0.0),
    )
    residual_t = (
        energy_cleaned_t.astype(jnp.float32) - theta[None, :] * margin_cleaned_t.astype(jnp.float32)
    ).astype(jnp.bfloat16)
    residual = residual_t.T
    return (residual[None], margin_pencil[None], energy_pencil[None])


def solution(mesh):
    placed = (
        P("cuts", None, "row"),
        P("cuts"),
        P("cuts", None),
        P("row", None, None),
        P("row", None, None),
        P("row", None),
    )
    return jax.shard_map(
        shards,
        mesh=mesh,
        in_specs=placed,
        out_specs=(P("cuts", None, "row"), P("cuts", None, None), P("cuts", None, None)),
        check_vma=False,
    )
```

```python
import functools

import jax
import jax.numpy as jnp
from jax import lax
from jax.experimental import pallas as pl
from jax.experimental.pallas import tpu as pltpu
from jax.experimental.layout import Layout, with_layout_constraint
from jax.sharding import PartitionSpec as P

WIN = 32
NNZ = 3
HALO = 2


def from_behind(block, axis, distance):
    devices = range(lax.axis_size(axis))
    route = [(i - distance, i) for i in devices if i - distance in devices]
    return lax.ppermute(block, axis, route)


def row_halos(cells, width):
    count = lax.axis_size("row")
    ends = count - 1
    head = cells[:width]
    tail = cells[cells.shape[0] - width :]
    lower = lax.ppermute(tail, "row", [(i, i + 1) for i in range(ends)])
    upper = lax.ppermute(head, "row", [(i + 1, i) for i in range(ends)])
    return lower, upper


def apply_kernel(shift_ref, x_hbm, lo_ref, hi_ref, *refs, group, blk, nmat):
    mats = refs[:nmat]
    outs = refs[nmat : 2 * nmat]
    xpad, sem = refs[2 * nmat], refs[2 * nmat + 1]
    g = pl.program_id(0)
    entries = x_hbm.shape[0]
    halo = HALO * blk

    @pl.when(g == 0)
    def _():
        copy = pltpu.make_async_copy(x_hbm, xpad.at[pl.ds(halo, entries)], sem.at[0])
        copy.start()
        xpad[pl.ds(0, halo), :] = lo_ref[...]
        xpad[pl.ds(halo + entries, halo), :] = hi_ref[...]
        copy.wait()

    def body(j, carry):
        row = g * group + j
        parts = []
        for k in range(NNZ):
            src = row + shift_ref[row * NNZ + k] + HALO
            start = pl.multiple_of(src * blk, 16)
            parts.append(xpad[pl.ds(start, blk), :])
        xs = jnp.concatenate(parts, axis=0)
        lhs = jnp.concatenate([m[j] for m in mats], axis=0) if nmat > 1 else mats[0][j]
        r = jnp.dot(lhs, xs, preferred_element_type=jnp.float32)
        for m in range(nmat):
            part = r[m * blk : (m + 1) * blk]
            outs[m][pl.ds(pl.multiple_of(j * blk, 16), blk), :] = part.astype(outs[m].dtype)
        return carry

    lax.fori_loop(0, group, body, 0, unroll=8)


def block_apply(matrices, shifts_flat, cells):
    entries, slots = cells.shape
    block_rows, blk, width = matrices[0].shape
    lower, upper = row_halos(cells, HALO * blk)
    group = 32 if block_rows % 32 == 0 else block_rows
    nmat = len(matrices)
    kernel = functools.partial(apply_kernel, group=group, blk=blk, nmat=nmat)
    mat_spec = pl.BlockSpec((group, blk, width), lambda g, s: (g, 0, 0))
    out_spec = pl.BlockSpec((group * blk, slots), lambda g, s: (g, 0))
    halo_spec = pl.BlockSpec((HALO * blk, slots), lambda g, s: (0, 0))
    grid_spec = pltpu.PrefetchScalarGridSpec(
        num_scalar_prefetch=1,
        grid=(block_rows // group,),
        in_specs=[pl.BlockSpec(memory_space=pl.ANY), halo_spec, halo_spec] + [mat_spec] * nmat,
        out_specs=[out_spec] * nmat,
        scratch_shapes=[
            pltpu.VMEM((entries + 2 * HALO * blk, slots), cells.dtype),
            pltpu.SemaphoreType.DMA((1,)),
        ],
    )
    return pl.pallas_call(
        kernel,
        grid_spec=grid_spec,
        out_shape=[jax.ShapeDtypeStruct((entries, slots), jnp.bfloat16)] * nmat,
        compiler_params=pltpu.CompilerParams(dimension_semantics=("arbitrary",)),
    )(shifts_flat, cells, lower, upper, *matrices)


def row_sum(part):
    count = lax.axis_size("row")
    here = lax.axis_index("row")
    got = [part] + [
        lax.ppermute(part, "row", [(i, (i + step) % count) for i in range(count)])
        for step in range(1, count)
    ]
    stacked = jnp.stack(got)
    order = (here - jnp.arange(count, dtype=jnp.int32)) % count
    by_source = jnp.take(stacked, order, axis=0)
    total = by_source[0]
    for r in range(1, count):
        total = total + by_source[r]
    return total


def tn_dot(a, b):
    return lax.dot_general(a, b, (((0,), (0,)), ((), ())), preferred_element_type=jnp.float32)


def shards(vectors, counts, offsets, margin_blocks, energy_blocks, block_columns):
    own_vectors = vectors[0]
    vector_count, entries = own_vectors.shape
    nmat_total = entries * lax.axis_size("row")
    block_rows = margin_blocks.shape[0]
    valid_mask = jnp.arange(vector_count, dtype=jnp.int32) < counts[0]
    window_rows = jnp.arange(WIN, dtype=jnp.int32)[:, None]
    lower_window = jnp.where(
        window_rows + offsets[0, 0] < counts[0],
        lax.dynamic_slice_in_dim(own_vectors, offsets[0, 0], WIN, 0),
        jnp.zeros((), own_vectors.dtype),
    )
    upper_window = jnp.where(
        window_rows + offsets[0, 1] < counts[0],
        lax.dynamic_slice_in_dim(own_vectors, offsets[0, 1], WIN, 0),
        jnp.zeros((), own_vectors.dtype),
    )
    own_blocks = lax.axis_index("row") * block_rows + jnp.arange(block_rows, dtype=jnp.int32)
    shifts_flat = (block_columns - own_blocks[:, None]).reshape(-1)
    from_below = [from_behind(upper_window, "cuts", distance) for distance in (2, 1)]
    from_above = [from_behind(lower_window, "cuts", -distance) for distance in (1, 2)]
    masked_t = jnp.where(valid_mask[None, :], own_vectors.T, jnp.zeros((), own_vectors.dtype))
    row_major = Layout(major_to_minor=(0, 1, 2))
    margin_blocks = with_layout_constraint(margin_blocks, row_major)
    energy_blocks = with_layout_constraint(energy_blocks, row_major)
    received, masked_t, margin_blocks, energy_blocks = lax.optimization_barrier(
        (from_below + from_above, masked_t, margin_blocks, energy_blocks)
    )
    windows_t = jnp.concatenate(received, axis=0).T
    (margin_windows_t,) = block_apply((margin_blocks,), shifts_flat, windows_t)
    partial_margin = tn_dot(margin_windows_t, masked_t)
    margin = row_sum(partial_margin) / nmat_total
    removed_t = jnp.dot(windows_t, margin.astype(jnp.bfloat16), preferred_element_type=jnp.float32)
    cleaned_t = (masked_t.astype(jnp.float32) - removed_t).astype(jnp.bfloat16)
    margin_cleaned_t, energy_cleaned_t = block_apply(
        (margin_blocks, energy_blocks), shifts_flat, cleaned_t
    )
    margin_part = tn_dot(cleaned_t, margin_cleaned_t)
    energy_part = tn_dot(cleaned_t, energy_cleaned_t)
    margin_total, energy_total = row_sum(jnp.stack([margin_part, energy_part]))
    margin_pencil = margin_total / nmat_total
    energy_pencil = energy_total / nmat_total
    margin_diag = jnp.diagonal(margin_pencil)
    energy_diag = jnp.diagonal(energy_pencil)
    theta = jnp.where(
        valid_mask,
        energy_diag / jnp.where(valid_mask, margin_diag, jnp.float32(1.0)),
        jnp.float32(0.0),
    )
    residual_t = (
        energy_cleaned_t.astype(jnp.float32) - theta[None, :] * margin_cleaned_t.astype(jnp.float32)
    ).astype(jnp.bfloat16)
    residual = residual_t.T
    return (residual[None], margin_pencil[None], energy_pencil[None])


def solution(mesh):
    placed = (
        P("cuts", None, "row"),
        P("cuts"),
        P("cuts", None),
        P("row", None, None),
        P("row", None, None),
        P("row", None),
    )
    return jax.shard_map(
        shards,
        mesh=mesh,
        in_specs=placed,
        out_specs=(P("cuts", None, "row"), P("cuts", None, None), P("cuts", None, None)),
        check_vma=False,
    )
```

```python
import functools

import jax
import jax.numpy as jnp
from jax import lax
from jax.experimental import pallas as pl
from jax.experimental.pallas import tpu as pltpu
from jax.experimental.layout import Layout, with_layout_constraint
from jax.sharding import PartitionSpec as P

WIN = 32
NNZ = 3
HALO = 2


def from_behind(block, axis, distance):
    devices = range(lax.axis_size(axis))
    route = [(i - distance, i) for i in devices if i - distance in devices]
    return lax.ppermute(block, axis, route)


def row_halos(cells, width):
    count = lax.axis_size("row")
    ends = count - 1
    head = cells[:, :width]
    tail = cells[:, cells.shape[1] - width :]
    lower = lax.ppermute(tail, "row", [(i, i + 1) for i in range(ends)])
    upper = lax.ppermute(head, "row", [(i + 1, i) for i in range(ends)])
    return lower, upper


def flip(tile):
    return tile.astype(jnp.float32).T.astype(jnp.bfloat16)


def apply_kernel(shift_ref, x_hbm, lo_ref, hi_ref, *refs, group, blk, nmat, chunk):
    mats = refs[:nmat]
    outs = refs[nmat : 2 * nmat]
    accs = refs[2 * nmat : 3 * nmat]
    xbuf, xpad, sem = refs[3 * nmat :]
    g = pl.program_id(0)
    entries = x_hbm.shape[1]
    halo = HALO * blk
    rim = lo_ref.shape[1]

    @pl.when(g == 0)
    def _():
        copy = pltpu.make_async_copy(x_hbm, xbuf, sem.at[0])
        copy.start()
        xpad[pl.ds(0, halo), :] = flip(lo_ref[...])[rim - halo :]
        xpad[pl.ds(halo + entries, halo), :] = flip(hi_ref[...])[:halo]
        copy.wait()

        def turn(c, carry):
            col = pl.multiple_of(c * chunk, chunk)
            xpad[pl.ds(halo + col, chunk), :] = flip(xbuf[:, pl.ds(col, chunk)])
            return carry

        lax.fori_loop(0, entries // chunk, turn, 0)

    def body(j, carry):
        row = g * group + j
        parts = []
        for k in range(NNZ):
            src = row + shift_ref[row * NNZ + k] + HALO
            start = pl.multiple_of(src * blk, 16)
            parts.append(xpad[pl.ds(start, blk), :])
        xs = jnp.concatenate(parts, axis=0)
        lhs = jnp.concatenate([m[j] for m in mats], axis=0) if nmat > 1 else mats[0][j]
        r = jnp.dot(lhs, xs, preferred_element_type=jnp.float32)
        for m in range(nmat):
            part = r[m * blk : (m + 1) * blk]
            accs[m][pl.ds(pl.multiple_of(j * blk, 16), blk), :] = part.astype(accs[m].dtype)
        return carry

    lax.fori_loop(0, group, body, 0, unroll=8)
    for m in range(nmat):
        for c in range(group * blk // chunk):
            outs[m][:, pl.ds(c * chunk, chunk)] = flip(accs[m][pl.ds(c * chunk, chunk), :])


def block_apply(matrices, shifts_flat, cells):
    slots, entries = cells.shape
    block_rows, blk, width = matrices[0].shape
    rim = 256
    lower, upper = row_halos(cells, rim)
    group = 32 if block_rows % 32 == 0 else block_rows
    chunk = 512
    nmat = len(matrices)
    kernel = functools.partial(apply_kernel, group=group, blk=blk, nmat=nmat, chunk=chunk)
    mat_spec = pl.BlockSpec((group, blk, width), lambda g, s: (g, 0, 0))
    out_spec = pl.BlockSpec((slots, group * blk), lambda g, s: (0, g))
    halo_spec = pl.BlockSpec((slots, rim), lambda g, s: (0, 0))
    grid_spec = pltpu.PrefetchScalarGridSpec(
        num_scalar_prefetch=1,
        grid=(block_rows // group,),
        in_specs=[pl.BlockSpec(memory_space=pl.ANY), halo_spec, halo_spec] + [mat_spec] * nmat,
        out_specs=[out_spec] * nmat,
        scratch_shapes=[pltpu.VMEM((group * blk, slots), jnp.bfloat16)] * nmat
        + [
            pltpu.VMEM((slots, entries), cells.dtype),
            pltpu.VMEM((entries + 2 * HALO * blk, slots), cells.dtype),
            pltpu.SemaphoreType.DMA((1,)),
        ],
    )
    return pl.pallas_call(
        kernel,
        grid_spec=grid_spec,
        out_shape=[jax.ShapeDtypeStruct((slots, entries), jnp.bfloat16)] * nmat,
        compiler_params=pltpu.CompilerParams(
            dimension_semantics=("arbitrary",), vmem_limit_bytes=56 * 1024 * 1024
        ),
    )(shifts_flat, cells, lower, upper, *matrices)


def row_sum(part):
    count = lax.axis_size("row")
    here = lax.axis_index("row")
    got = [part] + [
        lax.ppermute(part, "row", [(i, (i + step) % count) for i in range(count)])
        for step in range(1, count)
    ]
    stacked = jnp.stack(got)
    order = (here - jnp.arange(count, dtype=jnp.int32)) % count
    by_source = jnp.take(stacked, order, axis=0)
    total = by_source[0]
    for r in range(1, count):
        total = total + by_source[r]
    return total


def nt_dot(a, b):
    return lax.dot_general(a, b, (((1,), (1,)), ((), ())), preferred_element_type=jnp.float32)


def shards(vectors, counts, offsets, margin_blocks, energy_blocks, block_columns):
    own_vectors = vectors[0]
    vector_count, entries = own_vectors.shape
    nmat_total = entries * lax.axis_size("row")
    block_rows = margin_blocks.shape[0]
    valid_mask = jnp.arange(vector_count, dtype=jnp.int32) < counts[0]
    window_rows = jnp.arange(WIN, dtype=jnp.int32)[:, None]
    lower_window = jnp.where(
        window_rows + offsets[0, 0] < counts[0],
        lax.dynamic_slice_in_dim(own_vectors, offsets[0, 0], WIN, 0),
        jnp.zeros((), own_vectors.dtype),
    )
    upper_window = jnp.where(
        window_rows + offsets[0, 1] < counts[0],
        lax.dynamic_slice_in_dim(own_vectors, offsets[0, 1], WIN, 0),
        jnp.zeros((), own_vectors.dtype),
    )
    own_blocks = lax.axis_index("row") * block_rows + jnp.arange(block_rows, dtype=jnp.int32)
    shifts_flat = (block_columns - own_blocks[:, None]).reshape(-1)
    from_below = [from_behind(upper_window, "cuts", distance) for distance in (2, 1)]
    from_above = [from_behind(lower_window, "cuts", -distance) for distance in (1, 2)]
    row_major = Layout(major_to_minor=(0, 1, 2))
    margin_blocks = with_layout_constraint(margin_blocks, row_major)
    energy_blocks = with_layout_constraint(energy_blocks, row_major)
    received, margin_blocks, energy_blocks = lax.optimization_barrier(
        (from_below + from_above, margin_blocks, energy_blocks)
    )
    masked = jnp.where(valid_mask[:, None], own_vectors, jnp.zeros((), own_vectors.dtype))
    windows = jnp.concatenate(received, axis=0)
    (margin_windows,) = block_apply((margin_blocks,), shifts_flat, windows)
    partial_margin = nt_dot(margin_windows, masked)
    margin = row_sum(partial_margin) / nmat_total
    removed = lax.dot_general(
        margin.astype(jnp.bfloat16), windows, (((0,), (0,)), ((), ())), preferred_element_type=jnp.float32
    )
    cleaned = (masked.astype(jnp.float32) - removed).astype(jnp.bfloat16)
    margin_cleaned, energy_cleaned = block_apply((margin_blocks, energy_blocks), shifts_flat, cleaned)
    margin_part = nt_dot(cleaned, margin_cleaned)
    energy_part = nt_dot(cleaned, energy_cleaned)
    margin_total, energy_total = row_sum(jnp.stack([margin_part, energy_part]))
    margin_pencil = margin_total / nmat_total
    energy_pencil = energy_total / nmat_total
    margin_diag = jnp.diagonal(margin_pencil)
    energy_diag = jnp.diagonal(energy_pencil)
    theta = jnp.where(
        valid_mask,
        energy_diag / jnp.where(valid_mask, margin_diag, jnp.float32(1.0)),
        jnp.float32(0.0),
    )
    residual = (
        energy_cleaned.astype(jnp.float32) - theta[:, None] * margin_cleaned.astype(jnp.float32)
    ).astype(jnp.bfloat16)
    return (residual[None], margin_pencil[None], energy_pencil[None])


def solution(mesh):
    placed = (
        P("cuts", None, "row"),
        P("cuts"),
        P("cuts", None),
        P("row", None, None),
        P("row", None, None),
        P("row", None),
    )
    return jax.shard_map(
        shards,
        mesh=mesh,
        in_specs=placed,
        out_specs=(P("cuts", None, "row"), P("cuts", None, None), P("cuts", None, None)),
        check_vma=False,
    )
```

```python
import functools

import jax
import jax.numpy as jnp
from jax import lax
from jax.experimental import pallas as pl
from jax.experimental.pallas import tpu as pltpu
from jax.experimental.layout import Layout, with_layout_constraint
from jax.sharding import PartitionSpec as P

WIN = 32
NNZ = 3
HALO = 2


def from_behind(block, axis, distance):
    devices = range(lax.axis_size(axis))
    route = [(i - distance, i) for i in devices if i - distance in devices]
    return lax.ppermute(block, axis, route)


def row_halos(cells, width):
    count = lax.axis_size("row")
    ends = count - 1
    head = cells[:, :width]
    tail = cells[:, cells.shape[1] - width :]
    lower = lax.ppermute(tail, "row", [(i, i + 1) for i in range(ends)])
    upper = lax.ppermute(head, "row", [(i + 1, i) for i in range(ends)])
    return lower, upper


def flip(tile):
    return tile.astype(jnp.float32).T.astype(jnp.bfloat16)


def apply_kernel(shift_ref, x_hbm, lo_ref, hi_ref, *refs, group, blk, nmat, chunk):
    mats = refs[:nmat]
    outs = refs[nmat : 2 * nmat]
    accs = refs[2 * nmat : 3 * nmat]
    xbuf, xpad, sem = refs[3 * nmat :]
    g = pl.program_id(0)
    entries = x_hbm.shape[1]
    halo = HALO * blk
    rim = lo_ref.shape[1]

    @pl.when(g == 0)
    def _():
        copy = pltpu.make_async_copy(x_hbm, xbuf, sem.at[0])
        copy.start()
        xpad[pl.ds(0, halo), :] = flip(lo_ref[...])[rim - halo :]
        xpad[pl.ds(halo + entries, halo), :] = flip(hi_ref[...])[:halo]
        copy.wait()

        def turn(c, carry):
            col = pl.multiple_of(c * chunk, chunk)
            xpad[pl.ds(halo + col, chunk), :] = flip(xbuf[:, pl.ds(col, chunk)])
            return carry

        lax.fori_loop(0, entries // chunk, turn, 0)

    def body(j, carry):
        row = g * group + j
        parts = []
        for k in range(NNZ):
            src = row + shift_ref[row * NNZ + k] + HALO
            start = pl.multiple_of(src * blk, 16)
            parts.append(xpad[pl.ds(start, blk), :])
        xs = jnp.concatenate(parts, axis=0)
        lhs = jnp.concatenate([m[j] for m in mats], axis=0) if nmat > 1 else mats[0][j]
        r = jnp.dot(lhs, xs, preferred_element_type=jnp.float32)
        for m in range(nmat):
            part = r[m * blk : (m + 1) * blk]
            accs[m][pl.ds(pl.multiple_of(j * blk, 16), blk), :] = part.astype(accs[m].dtype)
        return carry

    lax.fori_loop(0, group, body, 0, unroll=8)
    for m in range(nmat):
        for c in range(group * blk // chunk):
            outs[m][:, pl.ds(c * chunk, chunk)] = flip(accs[m][pl.ds(c * chunk, chunk), :])


def block_apply(matrices, shifts_flat, cells):
    slots, entries = cells.shape
    block_rows, blk, width = matrices[0].shape
    rim = 256
    lower, upper = row_halos(cells, rim)
    group = 32 if block_rows % 32 == 0 else block_rows
    chunk = 512
    nmat = len(matrices)
    kernel = functools.partial(apply_kernel, group=group, blk=blk, nmat=nmat, chunk=chunk)
    mat_spec = pl.BlockSpec((group, blk, width), lambda g, s: (g, 0, 0))
    out_spec = pl.BlockSpec((slots, group * blk), lambda g, s: (0, g))
    halo_spec = pl.BlockSpec((slots, rim), lambda g, s: (0, 0))
    grid_spec = pltpu.PrefetchScalarGridSpec(
        num_scalar_prefetch=1,
        grid=(block_rows // group,),
        in_specs=[pl.BlockSpec(memory_space=pl.ANY), halo_spec, halo_spec] + [mat_spec] * nmat,
        out_specs=[out_spec] * nmat,
        scratch_shapes=[pltpu.VMEM((group * blk, slots), jnp.bfloat16)] * nmat
        + [
            pltpu.VMEM((slots, entries), cells.dtype),
            pltpu.VMEM((entries + 2 * HALO * blk, slots), cells.dtype),
            pltpu.SemaphoreType.DMA((1,)),
        ],
    )
    return pl.pallas_call(
        kernel,
        grid_spec=grid_spec,
        out_shape=[jax.ShapeDtypeStruct((slots, entries), jnp.bfloat16)] * nmat,
        compiler_params=pltpu.CompilerParams(
            dimension_semantics=("arbitrary",), vmem_limit_bytes=56 * 1024 * 1024
        ),
    )(shifts_flat, cells, lower, upper, *matrices)


def row_sum(part):
    count = lax.axis_size("row")
    here = lax.axis_index("row")
    got = [part] + [
        lax.ppermute(part, "row", [(i, (i + step) % count) for i in range(count)])
        for step in range(1, count)
    ]
    stacked = jnp.stack(got)
    order = (here - jnp.arange(count, dtype=jnp.int32)) % count
    by_source = jnp.take(stacked, order, axis=0)
    total = by_source[0]
    for r in range(1, count):
        total = total + by_source[r]
    return total


def nt_dot(a, b):
    return lax.dot_general(a, b, (((1,), (1,)), ((), ())), preferred_element_type=jnp.float32)


def shards(vectors, counts, offsets, margin_blocks, energy_blocks, block_columns):
    own_vectors = vectors[0]
    vector_count, entries = own_vectors.shape
    nmat_total = entries * lax.axis_size("row")
    block_rows = margin_blocks.shape[0]
    valid_mask = jnp.arange(vector_count, dtype=jnp.int32) < counts[0]
    window_rows = jnp.arange(WIN, dtype=jnp.int32)[:, None]
    lower_window = jnp.where(
        window_rows + offsets[0, 0] < counts[0],
        lax.dynamic_slice_in_dim(own_vectors, offsets[0, 0], WIN, 0),
        jnp.zeros((), own_vectors.dtype),
    )
    upper_window = jnp.where(
        window_rows + offsets[0, 1] < counts[0],
        lax.dynamic_slice_in_dim(own_vectors, offsets[0, 1], WIN, 0),
        jnp.zeros((), own_vectors.dtype),
    )
    own_blocks = lax.axis_index("row") * block_rows + jnp.arange(block_rows, dtype=jnp.int32)
    shifts_flat = (block_columns - own_blocks[:, None]).reshape(-1)
    cuts_count = lax.axis_size("cuts")
    odd = lax.axis_index("cuts") % 2 == 1
    evens = range(0, cuts_count, 2)
    odds = range(1, cuts_count, 2)
    upper_1 = from_behind(upper_window, "cuts", 1)
    lower_1 = from_behind(lower_window, "cuts", -1)
    upper_direct = lax.ppermute(upper_window, "cuts", [(i, i + 2) for i in evens if i + 2 < cuts_count])
    lower_direct = lax.ppermute(lower_window, "cuts", [(i, i - 2) for i in odds if i - 2 >= 0])
    row_major = Layout(major_to_minor=(0, 1, 2))
    margin_blocks = with_layout_constraint(margin_blocks, row_major)
    energy_blocks = with_layout_constraint(energy_blocks, row_major)
    upper_1, lower_1, upper_direct, lower_direct, margin_blocks, energy_blocks = lax.optimization_barrier(
        (upper_1, lower_1, upper_direct, lower_direct, margin_blocks, energy_blocks)
    )
    upper_2 = jnp.where(
        odd, lax.ppermute(upper_1, "cuts", [(i, i + 1) for i in evens if i + 1 < cuts_count]), upper_direct
    )
    lower_2 = jnp.where(odd, lower_direct, lax.ppermute(lower_1, "cuts", [(i, i - 1) for i in odds]))
    received = [upper_2, upper_1, lower_1, lower_2]
    masked = jnp.where(valid_mask[:, None], own_vectors, jnp.zeros((), own_vectors.dtype))
    windows = jnp.concatenate(received, axis=0)
    (margin_windows,) = block_apply((margin_blocks,), shifts_flat, windows)
    partial_margin = nt_dot(margin_windows, masked)
    margin = row_sum(partial_margin) / nmat_total
    removed = lax.dot_general(
        margin.astype(jnp.bfloat16), windows, (((0,), (0,)), ((), ())), preferred_element_type=jnp.float32
    )
    cleaned = (masked.astype(jnp.float32) - removed).astype(jnp.bfloat16)
    margin_cleaned, energy_cleaned = block_apply((margin_blocks, energy_blocks), shifts_flat, cleaned)
    margin_part = nt_dot(cleaned, margin_cleaned)
    energy_part = nt_dot(cleaned, energy_cleaned)
    margin_total, energy_total = row_sum(jnp.stack([margin_part, energy_part]))
    margin_pencil = margin_total / nmat_total
    energy_pencil = energy_total / nmat_total
    margin_diag = jnp.diagonal(margin_pencil)
    energy_diag = jnp.diagonal(energy_pencil)
    theta = jnp.where(
        valid_mask,
        energy_diag / jnp.where(valid_mask, margin_diag, jnp.float32(1.0)),
        jnp.float32(0.0),
    )
    residual = (
        energy_cleaned.astype(jnp.float32) - theta[:, None] * margin_cleaned.astype(jnp.float32)
    ).astype(jnp.bfloat16)
    return (residual[None], margin_pencil[None], energy_pencil[None])


def solution(mesh):
    placed = (
        P("cuts", None, "row"),
        P("cuts"),
        P("cuts", None),
        P("row", None, None),
        P("row", None, None),
        P("row", None),
    )
    return jax.shard_map(
        shards,
        mesh=mesh,
        in_specs=placed,
        out_specs=(P("cuts", None, "row"), P("cuts", None, None), P("cuts", None, None)),
        check_vma=False,
    )
```

```python
import functools

import jax
import jax.numpy as jnp
from jax import lax
from jax.experimental import pallas as pl
from jax.experimental.pallas import tpu as pltpu
from jax.experimental.layout import Layout, with_layout_constraint
from jax.sharding import PartitionSpec as P

WIN = 32
NNZ = 3
HALO = 2


def from_behind(block, axis, distance):
    devices = range(lax.axis_size(axis))
    route = [(i - distance, i) for i in devices if i - distance in devices]
    return lax.ppermute(block, axis, route)


def row_halos(cells, width):
    count = lax.axis_size("row")
    ends = count - 1
    head = cells[:, :width]
    tail = cells[:, cells.shape[1] - width :]
    lower = lax.ppermute(tail, "row", [(i, i + 1) for i in range(ends)])
    upper = lax.ppermute(head, "row", [(i + 1, i) for i in range(ends)])
    return lower, upper


def flip(tile):
    return tile.T


def nt(a, b):
    return lax.dot_general(a, b, (((1,), (1,)), ((), ())), preferred_element_type=jnp.float32)


def apply_kernel(shift_ref, count_ref, x_hbm, lo_ref, hi_ref, *refs, group, blk, nmat, chunk, keep, given):
    mats = refs[:nmat]
    at = nmat
    pair_ref = None
    if given:
        pair_ref = refs[at]
        at += 1
    outs = refs[at : at + nmat] if keep else ()
    at += nmat if keep else 0
    dots_ref = refs[at]
    accs = refs[at + 1 : at + 1 + nmat]
    xbuf, xpad, sem = refs[at + 1 + nmat :]
    g = pl.program_id(0)
    slots, entries = x_hbm.shape
    halo = HALO * blk
    rim = lo_ref.shape[1]
    span = group * blk

    @pl.when(g == 0)
    def _():
        copy = pltpu.make_async_copy(x_hbm, xbuf, sem.at[0])
        copy.start()
        xpad[pl.ds(0, halo), :] = flip(lo_ref[...])[rim - halo :]
        xpad[pl.ds(halo + entries, halo), :] = flip(hi_ref[...])[:halo]
        dots_ref[...] = jnp.zeros(dots_ref.shape, dots_ref.dtype)
        copy.wait()

        def turn(c, carry):
            col = pl.multiple_of(c * chunk, chunk)
            xpad[pl.ds(halo + col, chunk), :] = flip(xbuf[:, pl.ds(col, chunk)])
            return carry

        lax.fori_loop(0, entries // chunk, turn, 0)

    def body(j, carry):
        row = g * group + j
        parts = []
        for k in range(NNZ):
            src = row + shift_ref[row * NNZ + k] + HALO
            start = pl.multiple_of(src * blk, 16)
            parts.append(xpad[pl.ds(start, blk), :])
        xs = jnp.concatenate(parts, axis=0)
        lhs = jnp.concatenate([m[j] for m in mats], axis=0) if nmat > 1 else mats[0][j]
        r = jnp.dot(lhs, xs, preferred_element_type=jnp.float32)
        for m in range(nmat):
            part = r[m * blk : (m + 1) * blk]
            accs[m][pl.ds(pl.multiple_of(j * blk, 16), blk), :] = part.astype(accs[m].dtype)
        return carry

    lax.fori_loop(0, group, body, 0, unroll=16)
    live = lax.broadcasted_iota(jnp.int32, (slots, chunk), 0) < count_ref[0]
    for c in range(span // chunk):
        if given:
            other = jnp.where(live, pair_ref[:, pl.ds(c * chunk, chunk)], jnp.zeros((), pair_ref.dtype))
        else:
            other = xbuf[:, pl.ds(pl.multiple_of(g * span + c * chunk, chunk), chunk)]
        for m in range(nmat):
            native = flip(accs[m][pl.ds(c * chunk, chunk), :])
            if keep:
                outs[m][:, pl.ds(c * chunk, chunk)] = native
            if given:
                dots_ref[m] += nt(native, other)
            else:
                dots_ref[m] += nt(other, native)


def block_apply(matrices, shifts_flat, count, cells, pair=None):
    slots, entries = cells.shape
    block_rows, blk, width = matrices[0].shape
    rim = 256
    lower, upper = row_halos(cells, rim)
    group = 64 if block_rows % 64 == 0 else block_rows
    chunk = 512
    nmat = len(matrices)
    given = pair is not None
    keep = not given
    kernel = functools.partial(
        apply_kernel, group=group, blk=blk, nmat=nmat, chunk=chunk, keep=keep, given=given
    )
    mat_spec = pl.BlockSpec((group, blk, width), lambda g, s, n: (g, 0, 0))
    out_spec = pl.BlockSpec((slots, group * blk), lambda g, s, n: (0, g))
    halo_spec = pl.BlockSpec((slots, rim), lambda g, s, n: (0, 0))
    dots_spec = pl.BlockSpec((nmat, slots, slots), lambda g, s, n: (0, 0, 0))
    in_specs = [pl.BlockSpec(memory_space=pl.ANY), halo_spec, halo_spec] + [mat_spec] * nmat
    operands = [shifts_flat, count, cells, lower, upper, *matrices]
    if given:
        in_specs.append(out_spec)
        operands.append(pair)
    out_specs = ([out_spec] * nmat if keep else []) + [dots_spec]
    out_shape = ([jax.ShapeDtypeStruct((slots, entries), jnp.bfloat16)] * nmat if keep else []) + [
        jax.ShapeDtypeStruct((nmat, slots, slots), jnp.float32)
    ]
    grid_spec = pltpu.PrefetchScalarGridSpec(
        num_scalar_prefetch=2,
        grid=(block_rows // group,),
        in_specs=in_specs,
        out_specs=out_specs,
        scratch_shapes=[pltpu.VMEM((group * blk, slots), jnp.bfloat16)] * nmat
        + [
            pltpu.VMEM((slots, entries), cells.dtype),
            pltpu.VMEM((entries + 2 * HALO * blk, slots), cells.dtype),
            pltpu.SemaphoreType.DMA((1,)),
        ],
    )
    return pl.pallas_call(
        kernel,
        grid_spec=grid_spec,
        out_shape=out_shape,
        compiler_params=pltpu.CompilerParams(
            dimension_semantics=("arbitrary",), vmem_limit_bytes=56 * 1024 * 1024
        ),
    )(*operands)


def row_sum(part):
    count = lax.axis_size("row")
    if count & (count - 1):
        here = lax.axis_index("row")
        got = [part] + [
            lax.ppermute(part, "row", [(i, (i + step) % count) for i in range(count)])
            for step in range(1, count)
        ]
        by_source = jnp.take(jnp.stack(got), (here - jnp.arange(count, dtype=jnp.int32)) % count, axis=0)
        total = by_source[0]
        for r in range(1, count):
            total = total + by_source[r]
        return total
    step = 1
    while step < count:
        part = part + lax.ppermute(part, "row", [(i, i ^ step) for i in range(count)])
        step *= 2
    return part


def shards(vectors, counts, offsets, margin_blocks, energy_blocks, block_columns):
    own_vectors = vectors[0]
    vector_count, entries = own_vectors.shape
    nmat_total = entries * lax.axis_size("row")
    block_rows = margin_blocks.shape[0]
    valid_mask = jnp.arange(vector_count, dtype=jnp.int32) < counts[0]
    window_rows = jnp.arange(WIN, dtype=jnp.int32)[:, None]
    lower_window = jnp.where(
        window_rows + offsets[0, 0] < counts[0],
        lax.dynamic_slice_in_dim(own_vectors, offsets[0, 0], WIN, 0),
        jnp.zeros((), own_vectors.dtype),
    )
    upper_window = jnp.where(
        window_rows + offsets[0, 1] < counts[0],
        lax.dynamic_slice_in_dim(own_vectors, offsets[0, 1], WIN, 0),
        jnp.zeros((), own_vectors.dtype),
    )
    own_blocks = lax.axis_index("row") * block_rows + jnp.arange(block_rows, dtype=jnp.int32)
    shifts_flat = (block_columns - own_blocks[:, None]).reshape(-1)
    cuts_count = lax.axis_size("cuts")
    odd = lax.axis_index("cuts") % 2 == 1
    evens = range(0, cuts_count, 2)
    odds = range(1, cuts_count, 2)
    upper_1 = from_behind(upper_window, "cuts", 1)
    lower_1 = from_behind(lower_window, "cuts", -1)
    upper_direct = lax.ppermute(upper_window, "cuts", [(i, i + 2) for i in evens if i + 2 < cuts_count])
    lower_direct = lax.ppermute(lower_window, "cuts", [(i, i - 2) for i in odds if i - 2 >= 0])
    row_major = Layout(major_to_minor=(0, 1, 2))
    margin_blocks = with_layout_constraint(margin_blocks, row_major)
    energy_blocks = with_layout_constraint(energy_blocks, row_major)
    upper_1, lower_1, upper_direct, lower_direct, margin_blocks, energy_blocks = lax.optimization_barrier(
        (upper_1, lower_1, upper_direct, lower_direct, margin_blocks, energy_blocks)
    )
    upper_2 = jnp.where(
        odd, lax.ppermute(upper_1, "cuts", [(i, i + 1) for i in evens if i + 1 < cuts_count]), upper_direct
    )
    lower_2 = jnp.where(odd, lower_direct, lax.ppermute(lower_1, "cuts", [(i, i - 1) for i in odds]))
    received = [upper_2, upper_1, lower_1, lower_2]
    windows = jnp.concatenate(received, axis=0)
    count = counts[:1]
    (margin_dots,) = block_apply((margin_blocks,), shifts_flat, count, windows, pair=own_vectors)
    margin = row_sum(margin_dots[0]) / nmat_total
    removed = lax.dot_general(
        margin.astype(jnp.bfloat16), windows, (((0,), (0,)), ((), ())), preferred_element_type=jnp.float32
    )
    masked = jnp.where(valid_mask[:, None], own_vectors, jnp.zeros((), own_vectors.dtype))
    cleaned = (masked.astype(jnp.float32) - removed).astype(jnp.bfloat16)
    margin_cleaned, energy_cleaned, pencil_dots = block_apply(
        (margin_blocks, energy_blocks), shifts_flat, count, cleaned
    )
    pencils = row_sum(pencil_dots) / nmat_total
    margin_pencil = pencils[0]
    energy_pencil = pencils[1]
    margin_diag = jnp.diagonal(margin_pencil)
    energy_diag = jnp.diagonal(energy_pencil)
    theta = jnp.where(
        valid_mask,
        energy_diag / jnp.where(valid_mask, margin_diag, jnp.float32(1.0)),
        jnp.float32(0.0),
    )
    residual = (
        energy_cleaned.astype(jnp.float32) - theta[:, None] * margin_cleaned.astype(jnp.float32)
    ).astype(jnp.bfloat16)
    return (residual[None], margin_pencil[None], energy_pencil[None])


def solution(mesh):
    placed = (
        P("cuts", None, "row"),
        P("cuts"),
        P("cuts", None),
        P("row", None, None),
        P("row", None, None),
        P("row", None),
    )
    return jax.shard_map(
        shards,
        mesh=mesh,
        in_specs=placed,
        out_specs=(P("cuts", None, "row"), P("cuts", None, None), P("cuts", None, None)),
        check_vma=False,
    )
```

```python
import functools

import jax
import jax.numpy as jnp
from jax import lax
from jax.experimental import pallas as pl
from jax.experimental.pallas import tpu as pltpu
from jax.experimental.layout import Layout, with_layout_constraint
from jax.sharding import PartitionSpec as P

WIN = 32
NNZ = 3
HALO = 2


def from_behind(block, axis, distance):
    devices = range(lax.axis_size(axis))
    route = [(i - distance, i) for i in devices if i - distance in devices]
    return lax.ppermute(block, axis, route)


def row_halos(cells, width):
    count = lax.axis_size("row")
    ends = count - 1
    head = cells[:, :width]
    tail = cells[:, cells.shape[1] - width :]
    lower = lax.ppermute(tail, "row", [(i, i + 1) for i in range(ends)])
    upper = lax.ppermute(head, "row", [(i + 1, i) for i in range(ends)])
    return lower, upper


def flip(tile):
    return tile.T


def nt(a, b):
    return lax.dot_general(a, b, (((1,), (1,)), ((), ())), preferred_element_type=jnp.float32)


def apply_kernel(shift_ref, count_ref, x_hbm, lo_ref, hi_ref, *refs, group, blk, nmat, chunk, keep, given):
    mats = refs[:nmat]
    at = nmat
    pair_ref = None
    if given:
        pair_ref = refs[at]
        at += 1
    outs = refs[at : at + nmat] if keep else ()
    at += nmat if keep else 0
    dots_ref = refs[at]
    accs = refs[at + 1 : at + 1 + nmat]
    xbuf, xpad, sem = refs[at + 1 + nmat :]
    g = pl.program_id(0)
    slots, entries = x_hbm.shape
    halo = HALO * blk
    rim = lo_ref.shape[1]
    span = group * blk

    @pl.when(g == 0)
    def _():
        copy = pltpu.make_async_copy(x_hbm, xbuf, sem.at[0])
        copy.start()
        xpad[pl.ds(0, halo), :] = flip(lo_ref[...])[rim - halo :]
        xpad[pl.ds(halo + entries, halo), :] = flip(hi_ref[...])[:halo]
        dots_ref[...] = jnp.zeros(dots_ref.shape, dots_ref.dtype)
        copy.wait()

        def turn(c, carry):
            col = pl.multiple_of(c * chunk, chunk)
            xpad[pl.ds(halo + col, chunk), :] = flip(xbuf[:, pl.ds(col, chunk)])
            return carry

        lax.fori_loop(0, entries // chunk, turn, 0)

    def body(j, carry):
        row = g * group + j
        parts = []
        for k in range(NNZ):
            src = row + shift_ref[row * NNZ + k] + HALO
            start = pl.multiple_of(src * blk, 16)
            parts.append(xpad[pl.ds(start, blk), :])
        xs = jnp.concatenate(parts, axis=0)
        lhs = jnp.concatenate([m[j] for m in mats], axis=0) if nmat > 1 else mats[0][j]
        r = jnp.dot(lhs, xs, preferred_element_type=jnp.float32)
        for m in range(nmat):
            part = r[m * blk : (m + 1) * blk]
            accs[m][pl.ds(pl.multiple_of(j * blk, 16), blk), :] = part.astype(accs[m].dtype)
        return carry

    lax.fori_loop(0, group, body, 0, unroll=16)
    live = lax.broadcasted_iota(jnp.int32, (slots, chunk), 0) < count_ref[0]
    for c in range(span // chunk):
        if given:
            other = jnp.where(live, pair_ref[:, pl.ds(c * chunk, chunk)], jnp.zeros((), pair_ref.dtype))
        else:
            other = xbuf[:, pl.ds(pl.multiple_of(g * span + c * chunk, chunk), chunk)]
        for m in range(nmat):
            native = flip(accs[m][pl.ds(c * chunk, chunk), :])
            if keep:
                outs[m][:, pl.ds(c * chunk, chunk)] = native
            if given:
                dots_ref[m] += nt(native, other)
            else:
                dots_ref[m] += nt(other, native)


def block_apply(matrices, shifts_flat, count, cells, lower, upper, pair=None):
    slots, entries = cells.shape
    block_rows, blk, width = matrices[0].shape
    rim = lower.shape[1]
    group = 64 if block_rows % 64 == 0 else block_rows
    chunk = 512
    nmat = len(matrices)
    given = pair is not None
    keep = not given
    kernel = functools.partial(
        apply_kernel, group=group, blk=blk, nmat=nmat, chunk=chunk, keep=keep, given=given
    )
    mat_spec = pl.BlockSpec((group, blk, width), lambda g, s, n: (g, 0, 0))
    out_spec = pl.BlockSpec((slots, group * blk), lambda g, s, n: (0, g))
    halo_spec = pl.BlockSpec((slots, rim), lambda g, s, n: (0, 0))
    dots_spec = pl.BlockSpec((nmat, slots, slots), lambda g, s, n: (0, 0, 0))
    in_specs = [pl.BlockSpec(memory_space=pl.ANY), halo_spec, halo_spec] + [mat_spec] * nmat
    operands = [shifts_flat, count, cells, lower, upper, *matrices]
    if given:
        in_specs.append(out_spec)
        operands.append(pair)
    out_specs = ([out_spec] * nmat if keep else []) + [dots_spec]
    out_shape = ([jax.ShapeDtypeStruct((slots, entries), jnp.bfloat16)] * nmat if keep else []) + [
        jax.ShapeDtypeStruct((nmat, slots, slots), jnp.float32)
    ]
    grid_spec = pltpu.PrefetchScalarGridSpec(
        num_scalar_prefetch=2,
        grid=(block_rows // group,),
        in_specs=in_specs,
        out_specs=out_specs,
        scratch_shapes=[pltpu.VMEM((group * blk, slots), jnp.bfloat16)] * nmat
        + [
            pltpu.VMEM((slots, entries), cells.dtype),
            pltpu.VMEM((entries + 2 * HALO * blk, slots), cells.dtype),
            pltpu.SemaphoreType.DMA((1,)),
        ],
    )
    return pl.pallas_call(
        kernel,
        grid_spec=grid_spec,
        out_shape=out_shape,
        compiler_params=pltpu.CompilerParams(
            dimension_semantics=("arbitrary",), vmem_limit_bytes=56 * 1024 * 1024
        ),
    )(*operands)


def row_sum(part):
    count = lax.axis_size("row")
    if count & (count - 1):
        here = lax.axis_index("row")
        got = [part] + [
            lax.ppermute(part, "row", [(i, (i + step) % count) for i in range(count)])
            for step in range(1, count)
        ]
        by_source = jnp.take(jnp.stack(got), (here - jnp.arange(count, dtype=jnp.int32)) % count, axis=0)
        total = by_source[0]
        for r in range(1, count):
            total = total + by_source[r]
        return total
    step = 1
    while step < count:
        part = part + lax.ppermute(part, "row", [(i, i ^ step) for i in range(count)])
        step *= 2
    return part


def shards(vectors, counts, offsets, margin_blocks, energy_blocks, block_columns):
    own_vectors = vectors[0]
    vector_count, entries = own_vectors.shape
    nmat_total = entries * lax.axis_size("row")
    block_rows = margin_blocks.shape[0]
    valid_mask = jnp.arange(vector_count, dtype=jnp.int32) < counts[0]
    window_rows = jnp.arange(WIN, dtype=jnp.int32)[:, None]
    lower_window = jnp.where(
        window_rows + offsets[0, 0] < counts[0],
        lax.dynamic_slice_in_dim(own_vectors, offsets[0, 0], WIN, 0),
        jnp.zeros((), own_vectors.dtype),
    )
    upper_window = jnp.where(
        window_rows + offsets[0, 1] < counts[0],
        lax.dynamic_slice_in_dim(own_vectors, offsets[0, 1], WIN, 0),
        jnp.zeros((), own_vectors.dtype),
    )
    own_blocks = lax.axis_index("row") * block_rows + jnp.arange(block_rows, dtype=jnp.int32)
    shifts_flat = (block_columns - own_blocks[:, None]).reshape(-1)
    cuts_count = lax.axis_size("cuts")
    odd = lax.axis_index("cuts") % 2 == 1
    evens = range(0, cuts_count, 2)
    odds = range(1, cuts_count, 2)
    rim = 256

    def exchange(upper, lower):
        return (
            from_behind(upper, "cuts", 1),
            from_behind(lower, "cuts", -1),
            lax.ppermute(upper, "cuts", [(i, i + 2) for i in evens if i + 2 < cuts_count]),
            lax.ppermute(lower, "cuts", [(i, i - 2) for i in odds if i - 2 >= 0]),
        )

    def finish(upper_1, lower_1, upper_direct, lower_direct):
        upper_2 = jnp.where(
            odd, lax.ppermute(upper_1, "cuts", [(i, i + 1) for i in evens if i + 1 < cuts_count]), upper_direct
        )
        lower_2 = jnp.where(odd, lower_direct, lax.ppermute(lower_1, "cuts", [(i, i - 1) for i in odds]))
        return [upper_2, upper_1, lower_1, lower_2]

    masked = jnp.where(valid_mask[:, None], own_vectors, jnp.zeros((), own_vectors.dtype))
    below, above = row_halos(jnp.concatenate([upper_window, lower_window, masked], axis=0), rim)
    masked_lower, masked_upper = below[2 * WIN :], above[2 * WIN :]
    upper_ext = jnp.concatenate([upper_window, below[:WIN], above[:WIN]], axis=1)
    lower_ext = jnp.concatenate([lower_window, below[WIN : 2 * WIN], above[WIN : 2 * WIN]], axis=1)
    big = exchange(upper_ext, lower_ext)
    row_major = Layout(major_to_minor=(0, 1, 2))
    margin_blocks = with_layout_constraint(margin_blocks, row_major)
    energy_blocks = with_layout_constraint(energy_blocks, row_major)
    big, margin_blocks, energy_blocks = lax.optimization_barrier((big, margin_blocks, energy_blocks))
    received = jnp.concatenate(finish(*big), axis=0)
    windows = received[:, :entries]
    windows_lower = received[:, entries : entries + rim]
    windows_upper = received[:, entries + rim :]
    count = counts[:1]
    (margin_dots,) = block_apply(
        (margin_blocks,), shifts_flat, count, windows, windows_lower, windows_upper, pair=own_vectors
    )
    margin = row_sum(margin_dots[0]) / nmat_total
    margin_b = margin.astype(jnp.bfloat16)

    def clean(kept, wins):
        removed = lax.dot_general(margin_b, wins, (((0,), (0,)), ((), ())), preferred_element_type=jnp.float32)
        return (kept.astype(jnp.float32) - removed).astype(jnp.bfloat16)

    cleaned = clean(masked, windows)
    margin_cleaned, energy_cleaned, pencil_dots = block_apply(
        (margin_blocks, energy_blocks),
        shifts_flat,
        count,
        cleaned,
        clean(masked_lower, windows_lower),
        clean(masked_upper, windows_upper),
    )
    pencils = row_sum(pencil_dots) / nmat_total
    margin_pencil = pencils[0]
    energy_pencil = pencils[1]
    margin_diag = jnp.diagonal(margin_pencil)
    energy_diag = jnp.diagonal(energy_pencil)
    theta = jnp.where(
        valid_mask,
        energy_diag / jnp.where(valid_mask, margin_diag, jnp.float32(1.0)),
        jnp.float32(0.0),
    )
    residual = (
        energy_cleaned.astype(jnp.float32) - theta[:, None] * margin_cleaned.astype(jnp.float32)
    ).astype(jnp.bfloat16)
    return (residual[None], margin_pencil[None], energy_pencil[None])


def solution(mesh):
    placed = (
        P("cuts", None, "row"),
        P("cuts"),
        P("cuts", None),
        P("row", None, None),
        P("row", None, None),
        P("row", None),
    )
    return jax.shard_map(
        shards,
        mesh=mesh,
        in_specs=placed,
        out_specs=(P("cuts", None, "row"), P("cuts", None, None), P("cuts", None, None)),
        check_vma=False,
    )
```

```python
import functools

import jax
import jax.numpy as jnp
from jax import lax
from jax.experimental import pallas as pl
from jax.experimental.pallas import tpu as pltpu
from jax.experimental.layout import Layout, with_layout_constraint
from jax.sharding import PartitionSpec as P

WIN = 32
NNZ = 3
HALO = 2


def from_behind(block, axis, distance):
    devices = range(lax.axis_size(axis))
    route = [(i - distance, i) for i in devices if i - distance in devices]
    return lax.ppermute(block, axis, route)


def row_halos(cells, width):
    count = lax.axis_size("row")
    ends = count - 1
    head = cells[:, :width]
    tail = cells[:, cells.shape[1] - width :]
    lower = lax.ppermute(tail, "row", [(i, i + 1) for i in range(ends)])
    upper = lax.ppermute(head, "row", [(i + 1, i) for i in range(ends)])
    return lower, upper


def flip(tile):
    return tile.T


def nt(a, b):
    return lax.dot_general(a, b, (((1,), (1,)), ((), ())), preferred_element_type=jnp.float32)


def apply_kernel(shift_ref, count_ref, x_hbm, lo_ref, hi_ref, *refs, group, blk, nmat, chunk, keep, given):
    mats = refs[:nmat]
    at = nmat
    pair_ref = None
    if given:
        pair_ref = refs[at]
        at += 1
    outs = refs[at : at + nmat] if keep else ()
    at += nmat if keep else 0
    dots_ref = refs[at]
    accs = refs[at + 1 : at + 1 + nmat]
    xbuf, xpad, sem = refs[at + 1 + nmat :]
    g = pl.program_id(0)
    slots, entries = x_hbm.shape
    halo = HALO * blk
    rim = lo_ref.shape[1]
    span = group * blk

    @pl.when(g == 0)
    def _():
        pieces = sem.shape[0]
        piece = entries // pieces
        copies = [
            pltpu.make_async_copy(
                x_hbm.at[:, pl.ds(p * piece, piece)], xbuf.at[:, pl.ds(p * piece, piece)], sem.at[p]
            )
            for p in range(pieces)
        ]
        for copy in copies:
            copy.start()
        xpad[pl.ds(0, halo), :] = flip(lo_ref[...])[rim - halo :]
        xpad[pl.ds(halo + entries, halo), :] = flip(hi_ref[...])[:halo]
        dots_ref[...] = jnp.zeros(dots_ref.shape, dots_ref.dtype)

        def turn(c, carry):
            col = pl.multiple_of(c * chunk, chunk)
            xpad[pl.ds(halo + col, chunk), :] = flip(xbuf[:, pl.ds(col, chunk)])
            return carry

        for p in range(pieces):
            copies[p].wait()
            lax.fori_loop(p * piece // chunk, (p + 1) * piece // chunk, turn, 0)

    def body(j, carry):
        row = g * group + j
        parts = []
        for k in range(NNZ):
            src = row + shift_ref[row * NNZ + k] + HALO
            start = pl.multiple_of(src * blk, 16)
            parts.append(xpad[pl.ds(start, blk), :])
        xs = jnp.concatenate(parts, axis=0)
        lhs = jnp.concatenate([m[j] for m in mats], axis=0) if nmat > 1 else mats[0][j]
        r = jnp.dot(lhs, xs, preferred_element_type=jnp.float32)
        for m in range(nmat):
            part = r[m * blk : (m + 1) * blk]
            accs[m][pl.ds(pl.multiple_of(j * blk, 16), blk), :] = part.astype(accs[m].dtype)
        return carry

    lax.fori_loop(0, group, body, 0, unroll=16)
    live = lax.broadcasted_iota(jnp.int32, (slots, chunk), 0) < count_ref[0]
    for c in range(span // chunk):
        if given:
            other = jnp.where(live, pair_ref[:, pl.ds(c * chunk, chunk)], jnp.zeros((), pair_ref.dtype))
        else:
            other = xbuf[:, pl.ds(pl.multiple_of(g * span + c * chunk, chunk), chunk)]
        for m in range(nmat):
            native = flip(accs[m][pl.ds(c * chunk, chunk), :])
            if keep:
                outs[m][:, pl.ds(c * chunk, chunk)] = native
            if given:
                dots_ref[m] += nt(native, other)
            else:
                dots_ref[m] += nt(other, native)


def block_apply(matrices, shifts_flat, count, cells, lower, upper, pair=None):
    slots, entries = cells.shape
    block_rows, blk, width = matrices[0].shape
    rim = lower.shape[1]
    group = 64 if block_rows % 64 == 0 else block_rows
    chunk = 512
    nmat = len(matrices)
    given = pair is not None
    keep = not given
    kernel = functools.partial(
        apply_kernel, group=group, blk=blk, nmat=nmat, chunk=chunk, keep=keep, given=given
    )
    mat_spec = pl.BlockSpec((group, blk, width), lambda g, s, n: (g, 0, 0))
    out_spec = pl.BlockSpec((slots, group * blk), lambda g, s, n: (0, g))
    halo_spec = pl.BlockSpec((slots, rim), lambda g, s, n: (0, 0))
    dots_spec = pl.BlockSpec((nmat, slots, slots), lambda g, s, n: (0, 0, 0))
    in_specs = [pl.BlockSpec(memory_space=pl.ANY), halo_spec, halo_spec] + [mat_spec] * nmat
    operands = [shifts_flat, count, cells, lower, upper, *matrices]
    if given:
        in_specs.append(out_spec)
        operands.append(pair)
    out_specs = ([out_spec] * nmat if keep else []) + [dots_spec]
    out_shape = ([jax.ShapeDtypeStruct((slots, entries), jnp.bfloat16)] * nmat if keep else []) + [
        jax.ShapeDtypeStruct((nmat, slots, slots), jnp.float32)
    ]
    grid_spec = pltpu.PrefetchScalarGridSpec(
        num_scalar_prefetch=2,
        grid=(block_rows // group,),
        in_specs=in_specs,
        out_specs=out_specs,
        scratch_shapes=[pltpu.VMEM((group * blk, slots), jnp.bfloat16)] * nmat
        + [
            pltpu.VMEM((slots, entries), cells.dtype),
            pltpu.VMEM((entries + 2 * HALO * blk, slots), cells.dtype),
            pltpu.SemaphoreType.DMA((4 if entries % (4 * chunk) == 0 else 1,)),
        ],
    )
    return pl.pallas_call(
        kernel,
        grid_spec=grid_spec,
        out_shape=out_shape,
        compiler_params=pltpu.CompilerParams(
            dimension_semantics=("arbitrary",), vmem_limit_bytes=56 * 1024 * 1024
        ),
    )(*operands)


def row_sum(part):
    count = lax.axis_size("row")
    here = lax.axis_index("row")
    got = [part] + [
        lax.ppermute(part, "row", [(i, (i + step) % count) for i in range(count)])
        for step in range(1, count)
    ]
    stacked = jnp.stack(got)
    total = None
    for source in range(count):
        term = lax.dynamic_index_in_dim(stacked, (here - source) % count, 0, keepdims=False)
        total = term if total is None else total + term
    return total


def shards(vectors, counts, offsets, margin_blocks, energy_blocks, block_columns):
    own_vectors = vectors[0]
    vector_count, entries = own_vectors.shape
    nmat_total = entries * lax.axis_size("row")
    block_rows = margin_blocks.shape[0]
    valid_mask = jnp.arange(vector_count, dtype=jnp.int32) < counts[0]
    window_rows = jnp.arange(WIN, dtype=jnp.int32)[:, None]
    lower_window = jnp.where(
        window_rows + offsets[0, 0] < counts[0],
        lax.dynamic_slice_in_dim(own_vectors, offsets[0, 0], WIN, 0),
        jnp.zeros((), own_vectors.dtype),
    )
    upper_window = jnp.where(
        window_rows + offsets[0, 1] < counts[0],
        lax.dynamic_slice_in_dim(own_vectors, offsets[0, 1], WIN, 0),
        jnp.zeros((), own_vectors.dtype),
    )
    own_blocks = lax.axis_index("row") * block_rows + jnp.arange(block_rows, dtype=jnp.int32)
    shifts_flat = (block_columns - own_blocks[:, None]).reshape(-1)
    cuts_count = lax.axis_size("cuts")
    odd = lax.axis_index("cuts") % 2 == 1
    evens = range(0, cuts_count, 2)
    odds = range(1, cuts_count, 2)
    rim = 256

    def exchange(upper, lower):
        return (
            from_behind(upper, "cuts", 1),
            from_behind(lower, "cuts", -1),
            lax.ppermute(upper, "cuts", [(i, i + 2) for i in evens if i + 2 < cuts_count]),
            lax.ppermute(lower, "cuts", [(i, i - 2) for i in odds if i - 2 >= 0]),
        )

    def finish(upper_1, lower_1, upper_direct, lower_direct):
        upper_2 = jnp.where(
            odd, lax.ppermute(upper_1, "cuts", [(i, i + 1) for i in evens if i + 1 < cuts_count]), upper_direct
        )
        lower_2 = jnp.where(odd, lower_direct, lax.ppermute(lower_1, "cuts", [(i, i - 1) for i in odds]))
        return [upper_2, upper_1, lower_1, lower_2]

    masked = jnp.where(valid_mask[:, None], own_vectors, jnp.zeros((), own_vectors.dtype))
    below, above = row_halos(jnp.concatenate([upper_window, lower_window, masked], axis=0), rim)
    masked_lower, masked_upper = below[2 * WIN :], above[2 * WIN :]
    upper_ext = jnp.concatenate([upper_window, below[:WIN], above[:WIN]], axis=1)
    lower_ext = jnp.concatenate([lower_window, below[WIN : 2 * WIN], above[WIN : 2 * WIN]], axis=1)
    big = exchange(upper_ext, lower_ext)
    row_major = Layout(major_to_minor=(0, 1, 2))
    margin_blocks = with_layout_constraint(margin_blocks, row_major)
    energy_blocks = with_layout_constraint(energy_blocks, row_major)
    big, margin_blocks, energy_blocks = lax.optimization_barrier((big, margin_blocks, energy_blocks))
    received = jnp.concatenate(finish(*big), axis=0)
    windows = received[:, :entries]
    windows_lower = received[:, entries : entries + rim]
    windows_upper = received[:, entries + rim :]
    count = counts[:1]
    (margin_dots,) = block_apply(
        (margin_blocks,), shifts_flat, count, windows, windows_lower, windows_upper, pair=own_vectors
    )
    margin = row_sum(margin_dots[0]) / nmat_total
    margin_b = margin.astype(jnp.bfloat16)

    def clean(kept, wins):
        removed = lax.dot_general(margin_b, wins, (((0,), (0,)), ((), ())), preferred_element_type=jnp.float32)
        return (kept.astype(jnp.float32) - removed).astype(jnp.bfloat16)

    cleaned = clean(masked, windows)
    margin_cleaned, energy_cleaned, pencil_dots = block_apply(
        (margin_blocks, energy_blocks),
        shifts_flat,
        count,
        cleaned,
        clean(masked_lower, windows_lower),
        clean(masked_upper, windows_upper),
    )
    pencils = row_sum(pencil_dots) / nmat_total
    margin_pencil = pencils[0]
    energy_pencil = pencils[1]
    eye = jnp.arange(vector_count)[:, None] == jnp.arange(vector_count)[None, :]
    margin_diag = jnp.sum(jnp.where(eye, margin_pencil, 0.0), axis=1)
    energy_diag = jnp.sum(jnp.where(eye, energy_pencil, 0.0), axis=1)
    theta = jnp.where(
        valid_mask,
        energy_diag / jnp.where(valid_mask, margin_diag, jnp.float32(1.0)),
        jnp.float32(0.0),
    )
    residual = (
        energy_cleaned.astype(jnp.float32) - theta[:, None] * margin_cleaned.astype(jnp.float32)
    ).astype(jnp.bfloat16)
    return (residual[None], margin_pencil[None], energy_pencil[None])


def solution(mesh):
    placed = (
        P("cuts", None, "row"),
        P("cuts"),
        P("cuts", None),
        P("row", None, None),
        P("row", None, None),
        P("row", None),
    )
    return jax.shard_map(
        shards,
        mesh=mesh,
        in_specs=placed,
        out_specs=(P("cuts", None, "row"), P("cuts", None, None), P("cuts", None, None)),
        check_vma=False,
    )
```

```python
import functools

import jax
import jax.numpy as jnp
from jax import lax
from jax.experimental import pallas as pl
from jax.experimental.pallas import tpu as pltpu
from jax.experimental.layout import Layout, with_layout_constraint
from jax.sharding import PartitionSpec as P

WIN = 32
NNZ = 3
HALO = 2


def from_behind(block, axis, distance):
    devices = range(lax.axis_size(axis))
    route = [(i - distance, i) for i in devices if i - distance in devices]
    return lax.ppermute(block, axis, route)


def row_halos(cells, width):
    count = lax.axis_size("row")
    ends = count - 1
    head = cells[:, :width]
    tail = cells[:, cells.shape[1] - width :]
    lower = lax.ppermute(tail, "row", [(i, i + 1) for i in range(ends)])
    upper = lax.ppermute(head, "row", [(i + 1, i) for i in range(ends)])
    return lower, upper


def flip(tile):
    return tile.T


def nt(a, b):
    return lax.dot_general(a, b, (((1,), (1,)), ((), ())), preferred_element_type=jnp.float32)


def apply_kernel(shift_ref, count_ref, x_hbm, lo_ref, hi_ref, *refs, group, blk, nmat, chunk, keep, given):
    mats = refs[:nmat]
    at = nmat
    pair_ref = None
    if given:
        pair_ref = refs[at]
        at += 1
    outs = refs[at : at + nmat] if keep else ()
    at += nmat if keep else 0
    dots_ref = refs[at]
    accs = refs[at + 1 : at + 1 + nmat]
    xbuf, xpad, sem = refs[at + 1 + nmat :]
    g = pl.program_id(0)
    slots, entries = x_hbm.shape
    halo = HALO * blk
    rim = lo_ref.shape[1]
    span = group * blk

    @pl.when(g == 0)
    def _():
        pieces = sem.shape[0]
        piece = entries // pieces
        copies = [
            pltpu.make_async_copy(
                x_hbm.at[:, pl.ds(p * piece, piece)], xbuf.at[:, pl.ds(p * piece, piece)], sem.at[p]
            )
            for p in range(pieces)
        ]
        for copy in copies:
            copy.start()
        xpad[pl.ds(0, halo), :] = flip(lo_ref[...])[rim - halo :]
        xpad[pl.ds(halo + entries, halo), :] = flip(hi_ref[...])[:halo]
        dots_ref[...] = jnp.zeros(dots_ref.shape, dots_ref.dtype)

        def turn(c, carry):
            col = pl.multiple_of(c * chunk, chunk)
            xpad[pl.ds(halo + col, chunk), :] = flip(xbuf[:, pl.ds(col, chunk)])
            return carry

        for p in range(pieces):
            copies[p].wait()
            lax.fori_loop(p * piece // chunk, (p + 1) * piece // chunk, turn, 0)

    def body(j, carry):
        row = g * group + j
        parts = []
        for k in range(NNZ):
            src = row + shift_ref[row * NNZ + k] + HALO
            start = pl.multiple_of(src * blk, 16)
            parts.append(xpad[pl.ds(start, blk), :])
        xs = jnp.concatenate(parts, axis=0)
        lhs = jnp.concatenate([m[j] for m in mats], axis=0) if nmat > 1 else mats[0][j]
        r = jnp.dot(lhs, xs, preferred_element_type=jnp.float32)
        for m in range(nmat):
            part = r[m * blk : (m + 1) * blk]
            accs[m][pl.ds(pl.multiple_of(j * blk, 16), blk), :] = part.astype(accs[m].dtype)
        return carry

    lax.fori_loop(0, group, body, 0, unroll=16)
    live = lax.broadcasted_iota(jnp.int32, (slots, chunk), 0) < count_ref[0]
    for c in range(span // chunk):
        if given:
            other = jnp.where(live, pair_ref[:, pl.ds(c * chunk, chunk)], jnp.zeros((), pair_ref.dtype))
        else:
            other = xbuf[:, pl.ds(pl.multiple_of(g * span + c * chunk, chunk), chunk)]
        for m in range(nmat):
            native = flip(accs[m][pl.ds(c * chunk, chunk), :])
            if keep:
                outs[m][:, pl.ds(c * chunk, chunk)] = native
            if given:
                dots_ref[m] += nt(native, other)
            else:
                dots_ref[m] += nt(other, native)


def block_apply(matrices, shifts_flat, count, cells, lower, upper, pair=None):
    slots, entries = cells.shape
    block_rows, blk, width = matrices[0].shape
    rim = lower.shape[1]
    group = 64 if block_rows % 64 == 0 else block_rows
    chunk = 512
    nmat = len(matrices)
    given = pair is not None
    keep = not given
    kernel = functools.partial(
        apply_kernel, group=group, blk=blk, nmat=nmat, chunk=chunk, keep=keep, given=given
    )
    mat_spec = pl.BlockSpec((group, blk, width), lambda g, s, n: (g, 0, 0))
    out_spec = pl.BlockSpec((slots, group * blk), lambda g, s, n: (0, g))
    halo_spec = pl.BlockSpec((slots, rim), lambda g, s, n: (0, 0))
    dots_spec = pl.BlockSpec((nmat, slots, slots), lambda g, s, n: (0, 0, 0))
    in_specs = [pl.BlockSpec(memory_space=pl.ANY), halo_spec, halo_spec] + [mat_spec] * nmat
    operands = [shifts_flat, count, cells, lower, upper, *matrices]
    if given:
        in_specs.append(out_spec)
        operands.append(pair)
    out_specs = ([out_spec] * nmat if keep else []) + [dots_spec]
    out_shape = ([jax.ShapeDtypeStruct((slots, entries), jnp.bfloat16)] * nmat if keep else []) + [
        jax.ShapeDtypeStruct((nmat, slots, slots), jnp.float32)
    ]
    grid_spec = pltpu.PrefetchScalarGridSpec(
        num_scalar_prefetch=2,
        grid=(block_rows // group,),
        in_specs=in_specs,
        out_specs=out_specs,
        scratch_shapes=[pltpu.VMEM((group * blk, slots), jnp.bfloat16)] * nmat
        + [
            pltpu.VMEM((slots, entries), cells.dtype),
            pltpu.VMEM((entries + 2 * HALO * blk, slots), cells.dtype),
            pltpu.SemaphoreType.DMA((4 if entries % (4 * chunk) == 0 else 1,)),
        ],
    )
    return pl.pallas_call(
        kernel,
        grid_spec=grid_spec,
        out_shape=out_shape,
        compiler_params=pltpu.CompilerParams(
            dimension_semantics=("arbitrary",), vmem_limit_bytes=56 * 1024 * 1024
        ),
    )(*operands)


def row_sum(part):
    count = lax.axis_size("row")
    here = lax.axis_index("row")
    got = [part] + [
        lax.ppermute(part, "row", [(i, (i + step) % count) for i in range(count)])
        for step in range(1, count)
    ]
    stacked = jnp.stack(got)
    total = None
    for source in range(count):
        term = lax.dynamic_index_in_dim(stacked, (here - source) % count, 0, keepdims=False)
        total = term if total is None else total + term
    return total


def shards(vectors, counts, offsets, margin_blocks, energy_blocks, block_columns):
    own_vectors = vectors[0]
    vector_count, entries = own_vectors.shape
    nmat_total = entries * lax.axis_size("row")
    block_rows = margin_blocks.shape[0]
    valid_mask = jnp.arange(vector_count, dtype=jnp.int32) < counts[0]
    window_rows = jnp.arange(WIN, dtype=jnp.int32)[:, None]
    lower_window = jnp.where(
        window_rows + offsets[0, 0] < counts[0],
        lax.dynamic_slice_in_dim(own_vectors, offsets[0, 0], WIN, 0),
        jnp.zeros((), own_vectors.dtype),
    )
    upper_window = jnp.where(
        window_rows + offsets[0, 1] < counts[0],
        lax.dynamic_slice_in_dim(own_vectors, offsets[0, 1], WIN, 0),
        jnp.zeros((), own_vectors.dtype),
    )
    own_blocks = lax.axis_index("row") * block_rows + jnp.arange(block_rows, dtype=jnp.int32)
    shifts_flat = (block_columns - own_blocks[:, None]).reshape(-1)
    cuts_count = lax.axis_size("cuts")
    odd = lax.axis_index("cuts") % 2 == 1
    evens = range(0, cuts_count, 2)
    odds = range(1, cuts_count, 2)
    rim = 256

    def exchange(upper, lower):
        return (
            from_behind(upper, "cuts", 1),
            from_behind(lower, "cuts", -1),
            lax.ppermute(upper, "cuts", [(i, i + 2) for i in evens if i + 2 < cuts_count]),
            lax.ppermute(lower, "cuts", [(i, i - 2) for i in odds if i - 2 >= 0]),
        )

    def finish(upper_1, lower_1, upper_direct, lower_direct):
        upper_2 = jnp.where(
            odd, lax.ppermute(upper_1, "cuts", [(i, i + 1) for i in evens if i + 1 < cuts_count]), upper_direct
        )
        lower_2 = jnp.where(odd, lower_direct, lax.ppermute(lower_1, "cuts", [(i, i - 1) for i in odds]))
        return [upper_2, upper_1, lower_1, lower_2]

    masked = jnp.where(valid_mask[:, None], own_vectors, jnp.zeros((), own_vectors.dtype))

    def edge_rows(start, cols):
        rows = lax.dynamic_slice_in_dim(own_vectors[:, cols], start, WIN, 0)
        return jnp.where(window_rows + start < counts[0], rows, jnp.zeros((), rows.dtype))

    def edges_of(cols):
        return jnp.concatenate(
            [edge_rows(offsets[0, 1], cols), edge_rows(offsets[0, 0], cols), masked[:, cols]], axis=0
        )

    below = lax.ppermute(
        edges_of(slice(entries - rim, entries)), "row", [(i, i + 1) for i in range(lax.axis_size("row") - 1)]
    )
    above = lax.ppermute(edges_of(slice(0, rim)), "row", [(i + 1, i) for i in range(lax.axis_size("row") - 1)])
    masked_lower, masked_upper = below[2 * WIN :], above[2 * WIN :]
    upper_ext = jnp.concatenate([upper_window, below[:WIN], above[:WIN]], axis=1)
    lower_ext = jnp.concatenate([lower_window, below[WIN : 2 * WIN], above[WIN : 2 * WIN]], axis=1)
    big = exchange(upper_ext, lower_ext)
    row_major = Layout(major_to_minor=(0, 1, 2))
    margin_blocks = with_layout_constraint(margin_blocks, row_major)
    energy_blocks = with_layout_constraint(energy_blocks, row_major)
    big, margin_blocks, energy_blocks = lax.optimization_barrier((big, margin_blocks, energy_blocks))
    received = jnp.concatenate(finish(*big), axis=0)
    windows = received[:, :entries]
    windows_lower = received[:, entries : entries + rim]
    windows_upper = received[:, entries + rim :]
    count = counts[:1]
    (margin_dots,) = block_apply(
        (margin_blocks,), shifts_flat, count, windows, windows_lower, windows_upper, pair=own_vectors
    )
    margin = row_sum(margin_dots[0]) / nmat_total
    margin_b = margin.astype(jnp.bfloat16)

    def clean(kept, wins):
        removed = lax.dot_general(margin_b, wins, (((0,), (0,)), ((), ())), preferred_element_type=jnp.float32)
        return (kept.astype(jnp.float32) - removed).astype(jnp.bfloat16)

    cleaned = clean(masked, windows)
    margin_cleaned, energy_cleaned, pencil_dots = block_apply(
        (margin_blocks, energy_blocks),
        shifts_flat,
        count,
        cleaned,
        clean(masked_lower, windows_lower),
        clean(masked_upper, windows_upper),
    )
    eye = jnp.arange(vector_count)[:, None] == jnp.arange(vector_count)[None, :]
    diagonals = row_sum(jnp.sum(jnp.where(eye[None], pencil_dots, 0.0), axis=2)) / nmat_total
    margin_diag = diagonals[0]
    energy_diag = diagonals[1]
    pencils = row_sum(pencil_dots) / nmat_total
    margin_pencil = pencils[0]
    energy_pencil = pencils[1]
    theta = jnp.where(
        valid_mask,
        energy_diag / jnp.where(valid_mask, margin_diag, jnp.float32(1.0)),
        jnp.float32(0.0),
    )
    residual = (
        energy_cleaned.astype(jnp.float32) - theta[:, None] * margin_cleaned.astype(jnp.float32)
    ).astype(jnp.bfloat16)
    return (residual[None], margin_pencil[None], energy_pencil[None])


def solution(mesh):
    placed = (
        P("cuts", None, "row"),
        P("cuts"),
        P("cuts", None),
        P("row", None, None),
        P("row", None, None),
        P("row", None),
    )
    return jax.shard_map(
        shards,
        mesh=mesh,
        in_specs=placed,
        out_specs=(P("cuts", None, "row"), P("cuts", None, None), P("cuts", None, None)),
        check_vma=False,
    )
```

```python
import functools

import jax
import jax.numpy as jnp
from jax import lax
from jax.experimental import pallas as pl
from jax.experimental.pallas import tpu as pltpu
from jax.experimental.layout import Layout, with_layout_constraint
from jax.sharding import PartitionSpec as P

WIN = 32
NNZ = 3
HALO = 2


def from_behind(block, axis, distance):
    devices = range(lax.axis_size(axis))
    route = [(i - distance, i) for i in devices if i - distance in devices]
    return lax.ppermute(block, axis, route)


def row_halos(cells, width):
    count = lax.axis_size("row")
    ends = count - 1
    head = cells[:, :width]
    tail = cells[:, cells.shape[1] - width :]
    lower = lax.ppermute(tail, "row", [(i, i + 1) for i in range(ends)])
    upper = lax.ppermute(head, "row", [(i + 1, i) for i in range(ends)])
    return lower, upper


def flip(tile):
    return tile.T


def nt(a, b):
    return lax.dot_general(a, b, (((1,), (1,)), ((), ())), preferred_element_type=jnp.float32)


def apply_kernel(shift_ref, count_ref, x_hbm, lo_ref, hi_ref, *refs, group, blk, nmat, chunk, keep, given):
    mats = refs[:nmat]
    at = nmat
    pair_ref = None
    if given:
        pair_ref = refs[at]
        at += 1
    outs = refs[at : at + nmat] if keep else ()
    at += nmat if keep else 0
    dots_ref = refs[at]
    accs = refs[at + 1 : at + 1 + nmat]
    xbuf, xpad, sem = refs[at + 1 + nmat :]
    g = pl.program_id(0)
    slots, entries = x_hbm.shape
    halo = HALO * blk
    rim = lo_ref.shape[1]
    span = group * blk

    @pl.when(g == 0)
    def _():
        pieces = sem.shape[0]
        piece = entries // pieces
        copies = [
            pltpu.make_async_copy(
                x_hbm.at[:, pl.ds(p * piece, piece)], xbuf.at[:, pl.ds(p * piece, piece)], sem.at[p]
            )
            for p in range(pieces)
        ]
        for copy in copies:
            copy.start()
        xpad[pl.ds(0, halo), :] = flip(lo_ref[...])[rim - halo :]
        xpad[pl.ds(halo + entries, halo), :] = flip(hi_ref[...])[:halo]
        dots_ref[...] = jnp.zeros(dots_ref.shape, dots_ref.dtype)

        def turn(c, carry):
            col = pl.multiple_of(c * chunk, chunk)
            xpad[pl.ds(halo + col, chunk), :] = flip(xbuf[:, pl.ds(col, chunk)])
            return carry

        for p in range(pieces):
            copies[p].wait()
            lax.fori_loop(p * piece // chunk, (p + 1) * piece // chunk, turn, 0)

    def body(j, carry):
        row = g * group + j
        parts = []
        for k in range(NNZ):
            src = row + shift_ref[row * NNZ + k] + HALO
            start = pl.multiple_of(src * blk, 16)
            parts.append(xpad[pl.ds(start, blk), :])
        xs = jnp.concatenate(parts, axis=0)
        lhs = jnp.concatenate([m[j] for m in mats], axis=0) if nmat > 1 else mats[0][j]
        r = jnp.dot(lhs, xs, preferred_element_type=jnp.float32)
        for m in range(nmat):
            part = r[m * blk : (m + 1) * blk]
            accs[m][pl.ds(pl.multiple_of(j * blk, 16), blk), :] = part.astype(accs[m].dtype)
        return carry

    lax.fori_loop(0, group, body, 0, unroll=16)
    live = lax.broadcasted_iota(jnp.int32, (slots, chunk), 0) < count_ref[0]
    for c in range(span // chunk):
        if given:
            other = jnp.where(live, pair_ref[:, pl.ds(c * chunk, chunk)], jnp.zeros((), pair_ref.dtype))
        else:
            other = xbuf[:, pl.ds(pl.multiple_of(g * span + c * chunk, chunk), chunk)]
        for m in range(nmat):
            native = flip(accs[m][pl.ds(c * chunk, chunk), :])
            if keep:
                outs[m][:, pl.ds(c * chunk, chunk)] = native
            if given:
                dots_ref[m] += nt(native, other)
            else:
                dots_ref[m] += nt(other, native)


def block_apply(matrices, shifts_flat, count, cells, lower, upper, pair=None):
    slots, entries = cells.shape
    block_rows, blk, width = matrices[0].shape
    rim = lower.shape[1]
    group = 64 if block_rows % 64 == 0 else block_rows
    chunk = 512
    nmat = len(matrices)
    given = pair is not None
    keep = not given
    kernel = functools.partial(
        apply_kernel, group=group, blk=blk, nmat=nmat, chunk=chunk, keep=keep, given=given
    )
    mat_spec = pl.BlockSpec((group, blk, width), lambda g, s, n: (g, 0, 0))
    out_spec = pl.BlockSpec((slots, group * blk), lambda g, s, n: (0, g))
    halo_spec = pl.BlockSpec((slots, rim), lambda g, s, n: (0, 0))
    dots_spec = pl.BlockSpec((nmat, slots, slots), lambda g, s, n: (0, 0, 0))
    in_specs = [pl.BlockSpec(memory_space=pl.ANY), halo_spec, halo_spec] + [mat_spec] * nmat
    operands = [shifts_flat, count, cells, lower, upper, *matrices]
    if given:
        in_specs.append(out_spec)
        operands.append(pair)
    out_specs = ([out_spec] * nmat if keep else []) + [dots_spec]
    out_shape = ([jax.ShapeDtypeStruct((slots, entries), jnp.bfloat16)] * nmat if keep else []) + [
        jax.ShapeDtypeStruct((nmat, slots, slots), jnp.float32)
    ]
    grid_spec = pltpu.PrefetchScalarGridSpec(
        num_scalar_prefetch=2,
        grid=(block_rows // group,),
        in_specs=in_specs,
        out_specs=out_specs,
        scratch_shapes=[pltpu.VMEM((group * blk, slots), jnp.bfloat16)] * nmat
        + [
            pltpu.VMEM((slots, entries), cells.dtype),
            pltpu.VMEM((entries + 2 * HALO * blk, slots), cells.dtype),
            pltpu.SemaphoreType.DMA((4 if entries % (4 * chunk) == 0 else 1,)),
        ],
    )
    return pl.pallas_call(
        kernel,
        grid_spec=grid_spec,
        out_shape=out_shape,
        compiler_params=pltpu.CompilerParams(
            dimension_semantics=("arbitrary",), vmem_limit_bytes=56 * 1024 * 1024
        ),
    )(*operands)


def row_sum(part):
    count = lax.axis_size("row")
    here = lax.axis_index("row")
    got = [part] + [
        lax.ppermute(part, "row", [(i, (i + step) % count) for i in range(count)])
        for step in range(1, count)
    ]
    stacked = jnp.stack(got)
    total = None
    for source in range(count):
        term = lax.dynamic_index_in_dim(stacked, (here - source) % count, 0, keepdims=False)
        total = term if total is None else total + term
    return total


def shards(vectors, counts, offsets, margin_blocks, energy_blocks, block_columns):
    own_vectors = vectors[0]
    vector_count, entries = own_vectors.shape
    nmat_total = entries * lax.axis_size("row")
    block_rows = margin_blocks.shape[0]
    valid_mask = jnp.arange(vector_count, dtype=jnp.int32) < counts[0]
    window_rows = jnp.arange(WIN, dtype=jnp.int32)[:, None]
    lower_window = jnp.where(
        window_rows + offsets[0, 0] < counts[0],
        lax.dynamic_slice_in_dim(own_vectors, offsets[0, 0], WIN, 0),
        jnp.zeros((), own_vectors.dtype),
    )
    upper_window = jnp.where(
        window_rows + offsets[0, 1] < counts[0],
        lax.dynamic_slice_in_dim(own_vectors, offsets[0, 1], WIN, 0),
        jnp.zeros((), own_vectors.dtype),
    )
    own_blocks = lax.axis_index("row") * block_rows + jnp.arange(block_rows, dtype=jnp.int32)
    shifts_flat = (block_columns - own_blocks[:, None]).reshape(-1)
    cuts_count = lax.axis_size("cuts")
    odd = lax.axis_index("cuts") % 2 == 1
    evens = range(0, cuts_count, 2)
    odds = range(1, cuts_count, 2)
    rim = 256

    def exchange(upper, lower):
        return (
            from_behind(upper, "cuts", 1),
            from_behind(lower, "cuts", -1),
            lax.ppermute(upper, "cuts", [(i, i + 2) for i in evens if i + 2 < cuts_count]),
            lax.ppermute(lower, "cuts", [(i, i - 2) for i in odds if i - 2 >= 0]),
        )

    def finish(upper_1, lower_1, upper_direct, lower_direct):
        upper_2 = jnp.where(
            odd, lax.ppermute(upper_1, "cuts", [(i, i + 1) for i in evens if i + 1 < cuts_count]), upper_direct
        )
        lower_2 = jnp.where(odd, lower_direct, lax.ppermute(lower_1, "cuts", [(i, i - 1) for i in odds]))
        return [upper_2, upper_1, lower_1, lower_2]

    masked = jnp.where(valid_mask[:, None], own_vectors, jnp.zeros((), own_vectors.dtype))

    def edge_rows(start, cols):
        rows = lax.dynamic_slice_in_dim(own_vectors[:, cols], start, WIN, 0)
        return jnp.where(window_rows + start < counts[0], rows, jnp.zeros((), rows.dtype))

    def edges_of(cols):
        return jnp.concatenate(
            [edge_rows(offsets[0, 1], cols), edge_rows(offsets[0, 0], cols), masked[:, cols]], axis=0
        )

    big = exchange(upper_window, lower_window)
    row_major = Layout(major_to_minor=(0, 1, 2))
    margin_blocks = with_layout_constraint(margin_blocks, row_major)
    energy_blocks = with_layout_constraint(energy_blocks, row_major)
    below = lax.ppermute(
        edges_of(slice(entries - rim, entries)), "row", [(i, i + 1) for i in range(lax.axis_size("row") - 1)]
    )
    above = lax.ppermute(edges_of(slice(0, rim)), "row", [(i + 1, i) for i in range(lax.axis_size("row") - 1)])
    below, above, margin_blocks = lax.optimization_barrier((below, above, margin_blocks))
    masked_lower, masked_upper = below[2 * WIN :], above[2 * WIN :]
    upper_edges = jnp.concatenate([below[:WIN], above[:WIN]], axis=1)
    lower_edges = jnp.concatenate([below[WIN : 2 * WIN], above[WIN : 2 * WIN]], axis=1)
    small = exchange(upper_edges, lower_edges)
    big, small, energy_blocks = lax.optimization_barrier((big, small, energy_blocks))
    windows = jnp.concatenate(finish(*big), axis=0)
    edges = jnp.concatenate(finish(*small), axis=0)
    windows_lower = edges[:, :rim]
    windows_upper = edges[:, rim:]
    count = counts[:1]
    (margin_dots,) = block_apply(
        (margin_blocks,), shifts_flat, count, windows, windows_lower, windows_upper, pair=own_vectors
    )
    margin = row_sum(margin_dots[0]) / nmat_total
    margin_b = margin.astype(jnp.bfloat16)

    def clean(kept, wins):
        removed = lax.dot_general(margin_b, wins, (((0,), (0,)), ((), ())), preferred_element_type=jnp.float32)
        return (kept.astype(jnp.float32) - removed).astype(jnp.bfloat16)

    cleaned = clean(masked, windows)
    margin_cleaned, energy_cleaned, pencil_dots = block_apply(
        (margin_blocks, energy_blocks),
        shifts_flat,
        count,
        cleaned,
        clean(masked_lower, windows_lower),
        clean(masked_upper, windows_upper),
    )
    eye = jnp.arange(vector_count)[:, None] == jnp.arange(vector_count)[None, :]
    diagonals = row_sum(jnp.sum(jnp.where(eye[None], pencil_dots, 0.0), axis=2)) / nmat_total
    margin_diag = diagonals[0]
    energy_diag = diagonals[1]
    pencils = row_sum(pencil_dots) / nmat_total
    margin_pencil = pencils[0]
    energy_pencil = pencils[1]
    theta = jnp.where(
        valid_mask,
        energy_diag / jnp.where(valid_mask, margin_diag, jnp.float32(1.0)),
        jnp.float32(0.0),
    )
    residual = (
        energy_cleaned.astype(jnp.float32) - theta[:, None] * margin_cleaned.astype(jnp.float32)
    ).astype(jnp.bfloat16)
    return (residual[None], margin_pencil[None], energy_pencil[None])


def solution(mesh):
    placed = (
        P("cuts", None, "row"),
        P("cuts"),
        P("cuts", None),
        P("row", None, None),
        P("row", None, None),
        P("row", None),
    )
    return jax.shard_map(
        shards,
        mesh=mesh,
        in_specs=placed,
        out_specs=(P("cuts", None, "row"), P("cuts", None, None), P("cuts", None, None)),
        check_vma=False,
    )
```

```python
import functools

import jax
import jax.numpy as jnp
from jax import lax
from jax.experimental import pallas as pl
from jax.experimental.pallas import tpu as pltpu
from jax.experimental.layout import Layout, with_layout_constraint
from jax.sharding import PartitionSpec as P

WIN = 32
NNZ = 3
HALO = 2


def from_behind(block, axis, distance):
    devices = range(lax.axis_size(axis))
    route = [(i - distance, i) for i in devices if i - distance in devices]
    return lax.ppermute(block, axis, route)


def row_halos(cells, width):
    count = lax.axis_size("row")
    ends = count - 1
    head = cells[:, :width]
    tail = cells[:, cells.shape[1] - width :]
    lower = lax.ppermute(tail, "row", [(i, i + 1) for i in range(ends)])
    upper = lax.ppermute(head, "row", [(i + 1, i) for i in range(ends)])
    return lower, upper


def flip(tile):
    return tile.T


def nt(a, b):
    return lax.dot_general(a, b, (((1,), (1,)), ((), ())), preferred_element_type=jnp.float32)


def apply_kernel(shift_ref, count_ref, x_hbm, lo_ref, hi_ref, *refs, group, blk, nmat, chunk, keep, given):
    mats = refs[:nmat]
    at = nmat
    pair_ref = None
    if given:
        pair_ref = refs[at]
        at += 1
    outs = refs[at : at + nmat] if keep else ()
    at += nmat if keep else 0
    dots_ref = refs[at]
    accs = refs[at + 1 : at + 1 + nmat]
    xbuf, xpad, sem = refs[at + 1 + nmat :]
    g = pl.program_id(0)
    slots, entries = xbuf.shape
    halo = HALO * blk
    rim = lo_ref.shape[1]
    span = group * blk

    @pl.when(g == 0)
    def _():
        pieces = sem.shape[0]
        piece = entries // pieces
        copies = [
            pltpu.make_async_copy(
                x_hbm.at[:, pl.ds(p * piece, piece)], xbuf.at[:, pl.ds(p * piece, piece)], sem.at[p]
            )
            for p in range(pieces)
        ]
        for copy in copies:
            copy.start()
        xpad[pl.ds(0, halo), :] = flip(lo_ref[...])[rim - halo :]
        xpad[pl.ds(halo + entries, halo), :] = flip(hi_ref[...])[:halo]
        dots_ref[...] = jnp.zeros(dots_ref.shape, dots_ref.dtype)

        def turn(c, carry):
            col = pl.multiple_of(c * chunk, chunk)
            xpad[pl.ds(halo + col, chunk), :] = flip(xbuf[:, pl.ds(col, chunk)])
            return carry

        for p in range(pieces):
            copies[p].wait()
            lax.fori_loop(p * piece // chunk, (p + 1) * piece // chunk, turn, 0)

    def body(j, carry):
        row = g * group + j
        parts = []
        for k in range(NNZ):
            src = row + shift_ref[row * NNZ + k] + HALO
            start = pl.multiple_of(src * blk, 16)
            parts.append(xpad[pl.ds(start, blk), :])
        xs = jnp.concatenate(parts, axis=0)
        lhs = jnp.concatenate([m[j] for m in mats], axis=0) if nmat > 1 else mats[0][j]
        r = jnp.dot(lhs, xs, preferred_element_type=jnp.float32)
        for m in range(nmat):
            part = r[m * blk : (m + 1) * blk]
            accs[m][pl.ds(pl.multiple_of(j * blk, 16), blk), :] = part.astype(accs[m].dtype)
        return carry

    lax.fori_loop(0, group, body, 0, unroll=32)
    live = lax.broadcasted_iota(jnp.int32, (slots, chunk), 0) < count_ref[0]
    for c in range(span // chunk):
        if given:
            other = jnp.where(live, pair_ref[:, pl.ds(c * chunk, chunk)], jnp.zeros((), pair_ref.dtype))
        else:
            other = xbuf[:, pl.ds(pl.multiple_of(g * span + c * chunk, chunk), chunk)]
        for m in range(nmat):
            native = flip(accs[m][pl.ds(c * chunk, chunk), :])
            if keep:
                outs[m][:, pl.ds(c * chunk, chunk)] = native
            if given:
                dots_ref[m] += nt(native, other)
            else:
                dots_ref[m] += nt(other, native)


def block_apply(matrices, shifts_flat, count, cells, lower, upper, pair=None, entries=None):
    slots = cells.shape[0]
    entries = cells.shape[1] if entries is None else entries
    block_rows, blk, width = matrices[0].shape
    rim = lower.shape[1]
    group = 64 if block_rows % 64 == 0 else block_rows
    chunk = 512
    nmat = len(matrices)
    given = pair is not None
    keep = not given
    kernel = functools.partial(
        apply_kernel, group=group, blk=blk, nmat=nmat, chunk=chunk, keep=keep, given=given
    )
    mat_spec = pl.BlockSpec((group, blk, width), lambda g, s, n: (g, 0, 0))
    out_spec = pl.BlockSpec((slots, group * blk), lambda g, s, n: (0, g))
    halo_spec = pl.BlockSpec((slots, rim), lambda g, s, n: (0, 0))
    dots_spec = pl.BlockSpec((nmat, slots, slots), lambda g, s, n: (0, 0, 0))
    in_specs = [pl.BlockSpec(memory_space=pl.ANY), halo_spec, halo_spec] + [mat_spec] * nmat
    operands = [shifts_flat, count, cells, lower, upper, *matrices]
    if given:
        in_specs.append(out_spec)
        operands.append(pair)
    out_specs = ([out_spec] * nmat if keep else []) + [dots_spec]
    out_shape = ([jax.ShapeDtypeStruct((slots, entries), jnp.bfloat16)] * nmat if keep else []) + [
        jax.ShapeDtypeStruct((nmat, slots, slots), jnp.float32)
    ]
    grid_spec = pltpu.PrefetchScalarGridSpec(
        num_scalar_prefetch=2,
        grid=(block_rows // group,),
        in_specs=in_specs,
        out_specs=out_specs,
        scratch_shapes=[pltpu.VMEM((group * blk, slots), jnp.bfloat16)] * nmat
        + [
            pltpu.VMEM((slots, entries), cells.dtype),
            pltpu.VMEM((entries + 2 * HALO * blk, slots), cells.dtype),
            pltpu.SemaphoreType.DMA((4 if entries % (4 * chunk) == 0 else 1,)),
        ],
    )
    return pl.pallas_call(
        kernel,
        grid_spec=grid_spec,
        out_shape=out_shape,
        compiler_params=pltpu.CompilerParams(
            dimension_semantics=("arbitrary",), vmem_limit_bytes=56 * 1024 * 1024
        ),
    )(*operands)


def row_sum(part):
    count = lax.axis_size("row")
    here = lax.axis_index("row")
    got = [part] + [
        lax.ppermute(part, "row", [(i, (i + step) % count) for i in range(count)])
        for step in range(1, count)
    ]
    stacked = jnp.stack(got)
    total = None
    for source in range(count):
        term = lax.dynamic_index_in_dim(stacked, (here - source) % count, 0, keepdims=False)
        total = term if total is None else total + term
    return total


def shards(vectors, counts, offsets, margin_blocks, energy_blocks, block_columns):
    own_vectors = vectors[0]
    vector_count, entries = own_vectors.shape
    nmat_total = entries * lax.axis_size("row")
    block_rows = margin_blocks.shape[0]
    valid_mask = jnp.arange(vector_count, dtype=jnp.int32) < counts[0]
    window_rows = jnp.arange(WIN, dtype=jnp.int32)[:, None]
    lower_window = jnp.where(
        window_rows + offsets[0, 0] < counts[0],
        lax.dynamic_slice_in_dim(own_vectors, offsets[0, 0], WIN, 0),
        jnp.zeros((), own_vectors.dtype),
    )
    upper_window = jnp.where(
        window_rows + offsets[0, 1] < counts[0],
        lax.dynamic_slice_in_dim(own_vectors, offsets[0, 1], WIN, 0),
        jnp.zeros((), own_vectors.dtype),
    )
    own_blocks = lax.axis_index("row") * block_rows + jnp.arange(block_rows, dtype=jnp.int32)
    shifts_flat = (block_columns - own_blocks[:, None]).reshape(-1)
    cuts_count = lax.axis_size("cuts")
    odd = lax.axis_index("cuts") % 2 == 1
    evens = range(0, cuts_count, 2)
    odds = range(1, cuts_count, 2)
    rim = 256

    def exchange(upper, lower):
        return (
            from_behind(upper, "cuts", 1),
            from_behind(lower, "cuts", -1),
            lax.ppermute(upper, "cuts", [(i, i + 2) for i in evens if i + 2 < cuts_count]),
            lax.ppermute(lower, "cuts", [(i, i - 2) for i in odds if i - 2 >= 0]),
        )

    def finish(upper_1, lower_1, upper_direct, lower_direct):
        upper_2 = jnp.where(
            odd, lax.ppermute(upper_1, "cuts", [(i, i + 1) for i in evens if i + 1 < cuts_count]), upper_direct
        )
        lower_2 = jnp.where(odd, lower_direct, lax.ppermute(lower_1, "cuts", [(i, i - 1) for i in odds]))
        return [upper_2, upper_1, lower_1, lower_2]

    masked = jnp.where(valid_mask[:, None], own_vectors, jnp.zeros((), own_vectors.dtype))

    def edge_rows(start, cols):
        rows = lax.dynamic_slice_in_dim(own_vectors[:, cols], start, WIN, 0)
        return jnp.where(window_rows + start < counts[0], rows, jnp.zeros((), rows.dtype))

    def edges_of(cols):
        return jnp.concatenate(
            [edge_rows(offsets[0, 1], cols), edge_rows(offsets[0, 0], cols), masked[:, cols]], axis=0
        )

    below = lax.ppermute(
        edges_of(slice(entries - rim, entries)), "row", [(i, i + 1) for i in range(lax.axis_size("row") - 1)]
    )
    above = lax.ppermute(edges_of(slice(0, rim)), "row", [(i + 1, i) for i in range(lax.axis_size("row") - 1)])
    masked_lower, masked_upper = below[2 * WIN :], above[2 * WIN :]
    upper_ext = jnp.concatenate([upper_window, below[:WIN], above[:WIN]], axis=1)
    lower_ext = jnp.concatenate([lower_window, below[WIN : 2 * WIN], above[WIN : 2 * WIN]], axis=1)
    big = exchange(upper_ext, lower_ext)
    row_major = Layout(major_to_minor=(0, 1, 2))
    margin_blocks = with_layout_constraint(margin_blocks, row_major)
    energy_blocks = with_layout_constraint(energy_blocks, row_major)
    big, margin_blocks, energy_blocks = lax.optimization_barrier((big, margin_blocks, energy_blocks))
    received = jnp.concatenate(finish(*big), axis=0)
    windows = received[:, :entries]
    windows_lower = received[:, entries : entries + rim]
    windows_upper = received[:, entries + rim :]
    count = counts[:1]
    (margin_dots,) = block_apply(
        (margin_blocks,),
        shifts_flat,
        count,
        received,
        windows_lower,
        windows_upper,
        pair=own_vectors,
        entries=entries,
    )
    margin = row_sum(margin_dots[0]) / nmat_total
    margin_b = margin.astype(jnp.bfloat16)

    def clean(kept, wins):
        removed = lax.dot_general(margin_b, wins, (((0,), (0,)), ((), ())), preferred_element_type=jnp.float32)
        return (kept.astype(jnp.float32) - removed).astype(jnp.bfloat16)

    cleaned = clean(masked, windows)
    margin_cleaned, energy_cleaned, pencil_dots = block_apply(
        (margin_blocks, energy_blocks),
        shifts_flat,
        count,
        cleaned,
        clean(masked_lower, windows_lower),
        clean(masked_upper, windows_upper),
    )
    eye = jnp.arange(vector_count)[:, None] == jnp.arange(vector_count)[None, :]
    diagonals = row_sum(jnp.sum(jnp.where(eye[None], pencil_dots, 0.0), axis=2)) / nmat_total
    margin_diag = diagonals[0]
    energy_diag = diagonals[1]
    pencils = row_sum(pencil_dots) / nmat_total
    margin_pencil = pencils[0]
    energy_pencil = pencils[1]
    theta = jnp.where(
        valid_mask,
        energy_diag / jnp.where(valid_mask, margin_diag, jnp.float32(1.0)),
        jnp.float32(0.0),
    )
    residual = (
        energy_cleaned.astype(jnp.float32) - theta[:, None] * margin_cleaned.astype(jnp.float32)
    ).astype(jnp.bfloat16)
    return (residual[None], margin_pencil[None], energy_pencil[None])


def solution(mesh):
    placed = (
        P("cuts", None, "row"),
        P("cuts"),
        P("cuts", None),
        P("row", None, None),
        P("row", None, None),
        P("row", None),
    )
    return jax.shard_map(
        shards,
        mesh=mesh,
        in_specs=placed,
        out_specs=(P("cuts", None, "row"), P("cuts", None, None), P("cuts", None, None)),
        check_vma=False,
    )
```

```python
import functools

import jax
import jax.numpy as jnp
from jax import lax
from jax.experimental import pallas as pl
from jax.experimental.pallas import tpu as pltpu
from jax.experimental.layout import Layout, with_layout_constraint
from jax.sharding import PartitionSpec as P

WIN = 32
NNZ = 3
HALO = 2


def from_behind(block, axis, distance):
    devices = range(lax.axis_size(axis))
    route = [(i - distance, i) for i in devices if i - distance in devices]
    return lax.ppermute(block, axis, route)


def row_halos(cells, width):
    count = lax.axis_size("row")
    ends = count - 1
    head = cells[:, :width]
    tail = cells[:, cells.shape[1] - width :]
    lower = lax.ppermute(tail, "row", [(i, i + 1) for i in range(ends)])
    upper = lax.ppermute(head, "row", [(i + 1, i) for i in range(ends)])
    return lower, upper


def flip(tile):
    return tile.T


def nt(a, b):
    return lax.dot_general(a, b, (((1,), (1,)), ((), ())), preferred_element_type=jnp.float32)


def apply_kernel(shift_ref, count_ref, x_hbm, lo_ref, hi_ref, *refs, group, blk, nmat, chunk, keep, given):
    mats = refs[:nmat]
    at = nmat
    pair_ref = None
    if given:
        pair_ref = refs[at]
        at += 1
    outs = refs[at : at + nmat] if keep else ()
    at += nmat if keep else 0
    dots_ref = refs[at]
    accs = refs[at + 1 : at + 1 + nmat]
    xbuf, xpad, sem = refs[at + 1 + nmat :]
    g = pl.program_id(0)
    slots, entries = x_hbm.shape
    halo = HALO * blk
    rim = lo_ref.shape[1]
    span = group * blk

    @pl.when(g == 0)
    def _():
        pieces = sem.shape[0]
        piece = entries // pieces
        copies = [
            pltpu.make_async_copy(
                x_hbm.at[:, pl.ds(p * piece, piece)], xbuf.at[:, pl.ds(p * piece, piece)], sem.at[p]
            )
            for p in range(pieces)
        ]
        for copy in copies:
            copy.start()
        xpad[pl.ds(0, halo), :] = flip(lo_ref[...])[rim - halo :]
        xpad[pl.ds(halo + entries, halo), :] = flip(hi_ref[...])[:halo]
        dots_ref[...] = jnp.zeros(dots_ref.shape, dots_ref.dtype)

        def turn(c, carry):
            col = pl.multiple_of(c * chunk, chunk)
            xpad[pl.ds(halo + col, chunk), :] = flip(xbuf[:, pl.ds(col, chunk)])
            return carry

        for p in range(pieces):
            copies[p].wait()
            lax.fori_loop(p * piece // chunk, (p + 1) * piece // chunk, turn, 0)

    def body(j, carry):
        row = g * group + j
        parts = []
        for k in range(NNZ):
            src = row + shift_ref[row * NNZ + k] + HALO
            start = pl.multiple_of(src * blk, 16)
            parts.append(xpad[pl.ds(start, blk), :])
        xs = jnp.concatenate(parts, axis=0)
        lhs = jnp.concatenate([m[j] for m in mats], axis=0) if nmat > 1 else mats[0][j]
        r = jnp.dot(lhs, xs, preferred_element_type=jnp.float32)
        for m in range(nmat):
            part = r[m * blk : (m + 1) * blk]
            accs[m][pl.ds(pl.multiple_of(j * blk, 16), blk), :] = part.astype(accs[m].dtype)
        return carry

    lax.fori_loop(0, group, body, 0, unroll=16)
    live = lax.broadcasted_iota(jnp.int32, (slots, chunk), 0) < count_ref[0]
    for c in range(span // chunk):
        if given:
            other = jnp.where(live, pair_ref[:, pl.ds(c * chunk, chunk)], jnp.zeros((), pair_ref.dtype))
        else:
            other = xbuf[:, pl.ds(pl.multiple_of(g * span + c * chunk, chunk), chunk)]
        for m in range(nmat):
            native = flip(accs[m][pl.ds(c * chunk, chunk), :])
            if keep:
                outs[m][:, pl.ds(c * chunk, chunk)] = native
            if given:
                dots_ref[m] += nt(native, other)
            else:
                dots_ref[m] += nt(other, native)


def block_apply(matrices, shifts_flat, count, cells, lower, upper, pair=None):
    slots, entries = cells.shape
    block_rows, blk, width = matrices[0].shape
    rim = lower.shape[1]
    group = 32 if block_rows % 32 == 0 else block_rows
    chunk = 512
    nmat = len(matrices)
    given = pair is not None
    keep = not given
    kernel = functools.partial(
        apply_kernel, group=group, blk=blk, nmat=nmat, chunk=chunk, keep=keep, given=given
    )
    mat_spec = pl.BlockSpec((group, blk, width), lambda g, s, n: (g, 0, 0))
    out_spec = pl.BlockSpec((slots, group * blk), lambda g, s, n: (0, g))
    halo_spec = pl.BlockSpec((slots, rim), lambda g, s, n: (0, 0))
    dots_spec = pl.BlockSpec((nmat, slots, slots), lambda g, s, n: (0, 0, 0))
    in_specs = [pl.BlockSpec(memory_space=pl.ANY), halo_spec, halo_spec] + [mat_spec] * nmat
    operands = [shifts_flat, count, cells, lower, upper, *matrices]
    if given:
        in_specs.append(out_spec)
        operands.append(pair)
    out_specs = ([out_spec] * nmat if keep else []) + [dots_spec]
    out_shape = ([jax.ShapeDtypeStruct((slots, entries), jnp.bfloat16)] * nmat if keep else []) + [
        jax.ShapeDtypeStruct((nmat, slots, slots), jnp.float32)
    ]
    grid_spec = pltpu.PrefetchScalarGridSpec(
        num_scalar_prefetch=2,
        grid=(block_rows // group,),
        in_specs=in_specs,
        out_specs=out_specs,
        scratch_shapes=[pltpu.VMEM((group * blk, slots), jnp.bfloat16)] * nmat
        + [
            pltpu.VMEM((slots, entries), cells.dtype),
            pltpu.VMEM((entries + 2 * HALO * blk, slots), cells.dtype),
            pltpu.SemaphoreType.DMA((4 if entries % (4 * chunk) == 0 else 1,)),
        ],
    )
    return pl.pallas_call(
        kernel,
        grid_spec=grid_spec,
        out_shape=out_shape,
        compiler_params=pltpu.CompilerParams(
            dimension_semantics=("arbitrary",), vmem_limit_bytes=56 * 1024 * 1024
        ),
    )(*operands)


def row_sum(part):
    count = lax.axis_size("row")
    here = lax.axis_index("row")
    got = [part] + [
        lax.ppermute(part, "row", [(i, (i + step) % count) for i in range(count)])
        for step in range(1, count)
    ]
    stacked = jnp.stack(got)
    total = None
    for source in range(count):
        term = lax.dynamic_index_in_dim(stacked, (here - source) % count, 0, keepdims=False)
        total = term if total is None else total + term
    return total


def shards(vectors, counts, offsets, margin_blocks, energy_blocks, block_columns):
    own_vectors = vectors[0]
    vector_count, entries = own_vectors.shape
    nmat_total = entries * lax.axis_size("row")
    block_rows = margin_blocks.shape[0]
    valid_mask = jnp.arange(vector_count, dtype=jnp.int32) < counts[0]
    window_rows = jnp.arange(WIN, dtype=jnp.int32)[:, None]
    lower_window = jnp.where(
        window_rows + offsets[0, 0] < counts[0],
        lax.dynamic_slice_in_dim(own_vectors, offsets[0, 0], WIN, 0),
        jnp.zeros((), own_vectors.dtype),
    )
    upper_window = jnp.where(
        window_rows + offsets[0, 1] < counts[0],
        lax.dynamic_slice_in_dim(own_vectors, offsets[0, 1], WIN, 0),
        jnp.zeros((), own_vectors.dtype),
    )
    own_blocks = lax.axis_index("row") * block_rows + jnp.arange(block_rows, dtype=jnp.int32)
    shifts_flat = (block_columns - own_blocks[:, None]).reshape(-1)
    cuts_count = lax.axis_size("cuts")
    odd = lax.axis_index("cuts") % 2 == 1
    evens = range(0, cuts_count, 2)
    odds = range(1, cuts_count, 2)
    rim = 256

    def exchange(upper, lower):
        return (
            from_behind(upper, "cuts", 1),
            from_behind(lower, "cuts", -1),
            lax.ppermute(upper, "cuts", [(i, i + 2) for i in evens if i + 2 < cuts_count]),
            lax.ppermute(lower, "cuts", [(i, i - 2) for i in odds if i - 2 >= 0]),
        )

    def finish(upper_1, lower_1, upper_direct, lower_direct):
        upper_2 = jnp.where(
            odd, lax.ppermute(upper_1, "cuts", [(i, i + 1) for i in evens if i + 1 < cuts_count]), upper_direct
        )
        lower_2 = jnp.where(odd, lower_direct, lax.ppermute(lower_1, "cuts", [(i, i - 1) for i in odds]))
        return [upper_2, upper_1, lower_1, lower_2]

    masked = jnp.where(valid_mask[:, None], own_vectors, jnp.zeros((), own_vectors.dtype))

    def edge_rows(start, cols):
        rows = lax.dynamic_slice_in_dim(own_vectors[:, cols], start, WIN, 0)
        return jnp.where(window_rows + start < counts[0], rows, jnp.zeros((), rows.dtype))

    def edges_of(cols):
        return jnp.concatenate(
            [edge_rows(offsets[0, 1], cols), edge_rows(offsets[0, 0], cols), masked[:, cols]], axis=0
        )

    below = lax.ppermute(
        edges_of(slice(entries - rim, entries)), "row", [(i, i + 1) for i in range(lax.axis_size("row") - 1)]
    )
    above = lax.ppermute(edges_of(slice(0, rim)), "row", [(i + 1, i) for i in range(lax.axis_size("row") - 1)])
    masked_lower, masked_upper = below[2 * WIN :], above[2 * WIN :]
    upper_ext = jnp.concatenate([upper_window, below[:WIN], above[:WIN]], axis=1)
    lower_ext = jnp.concatenate([lower_window, below[WIN : 2 * WIN], above[WIN : 2 * WIN]], axis=1)
    big = exchange(upper_ext, lower_ext)
    row_major = Layout(major_to_minor=(0, 1, 2))
    margin_blocks = with_layout_constraint(margin_blocks, row_major)
    energy_blocks = with_layout_constraint(energy_blocks, row_major)
    big, margin_blocks, energy_blocks = lax.optimization_barrier((big, margin_blocks, energy_blocks))
    received = jnp.concatenate(finish(*big), axis=0)
    windows = received[:, :entries]
    windows_lower = received[:, entries : entries + rim]
    windows_upper = received[:, entries + rim :]
    count = counts[:1]
    (margin_dots,) = block_apply(
        (margin_blocks,), shifts_flat, count, windows, windows_lower, windows_upper, pair=own_vectors
    )
    margin = row_sum(margin_dots[0]) / nmat_total
    margin_b = margin.astype(jnp.bfloat16)

    def clean(kept, wins):
        removed = lax.dot_general(margin_b, wins, (((0,), (0,)), ((), ())), preferred_element_type=jnp.float32)
        return (kept.astype(jnp.float32) - removed).astype(jnp.bfloat16)

    cleaned = clean(masked, windows)
    margin_cleaned, energy_cleaned, pencil_dots = block_apply(
        (margin_blocks, energy_blocks),
        shifts_flat,
        count,
        cleaned,
        clean(masked_lower, windows_lower),
        clean(masked_upper, windows_upper),
    )
    eye = jnp.arange(vector_count)[:, None] == jnp.arange(vector_count)[None, :]
    diagonals = row_sum(jnp.sum(jnp.where(eye[None], pencil_dots, 0.0), axis=2)) / nmat_total
    margin_diag = diagonals[0]
    energy_diag = diagonals[1]
    pencils = row_sum(pencil_dots) / nmat_total
    margin_pencil = pencils[0]
    energy_pencil = pencils[1]
    theta = jnp.where(
        valid_mask,
        energy_diag / jnp.where(valid_mask, margin_diag, jnp.float32(1.0)),
        jnp.float32(0.0),
    )
    residual = (
        energy_cleaned.astype(jnp.float32) - theta[:, None] * margin_cleaned.astype(jnp.float32)
    ).astype(jnp.bfloat16)
    return (residual[None], margin_pencil[None], energy_pencil[None])


def solution(mesh):
    placed = (
        P("cuts", None, "row"),
        P("cuts"),
        P("cuts", None),
        P("row", None, None),
        P("row", None, None),
        P("row", None),
    )
    return jax.shard_map(
        shards,
        mesh=mesh,
        in_specs=placed,
        out_specs=(P("cuts", None, "row"), P("cuts", None, None), P("cuts", None, None)),
        check_vma=False,
    )
```

```python
import functools

import jax
import jax.numpy as jnp
from jax import lax
from jax.experimental import pallas as pl
from jax.experimental.pallas import tpu as pltpu
from jax.experimental.layout import Layout, with_layout_constraint
from jax.sharding import PartitionSpec as P

WIN = 32
NNZ = 3
HALO = 2


def from_behind(block, axis, distance):
    devices = range(lax.axis_size(axis))
    route = [(i - distance, i) for i in devices if i - distance in devices]
    return lax.ppermute(block, axis, route)


def row_halos(cells, width):
    count = lax.axis_size("row")
    ends = count - 1
    head = cells[:, :width]
    tail = cells[:, cells.shape[1] - width :]
    lower = lax.ppermute(tail, "row", [(i, i + 1) for i in range(ends)])
    upper = lax.ppermute(head, "row", [(i + 1, i) for i in range(ends)])
    return lower, upper


def flip(tile):
    return tile.T


def nt(a, b):
    return lax.dot_general(a, b, (((1,), (1,)), ((), ())), preferred_element_type=jnp.float32)


def apply_kernel(shift_ref, count_ref, x_hbm, lo_ref, hi_ref, *refs, group, blk, nmat, chunk, keep, given):
    mats = refs[:nmat]
    at = nmat
    pair_ref = None
    if given:
        pair_ref = refs[at]
        at += 1
    outs = refs[at : at + nmat] if keep else ()
    at += nmat if keep else 0
    dots_ref = refs[at]
    accs = refs[at + 1 : at + 1 + nmat]
    xbuf, xpad, sem = refs[at + 1 + nmat :]
    g = pl.program_id(0)
    slots, entries = x_hbm.shape
    halo = HALO * blk
    rim = lo_ref.shape[1]
    span = group * blk

    @pl.when(g == 0)
    def _():
        pieces = sem.shape[0]
        piece = entries // pieces
        copies = [
            pltpu.make_async_copy(
                x_hbm.at[:, pl.ds(p * piece, piece)], xbuf.at[:, pl.ds(p * piece, piece)], sem.at[p]
            )
            for p in range(pieces)
        ]
        for copy in copies:
            copy.start()
        xpad[pl.ds(0, halo), :] = flip(lo_ref[...])[rim - halo :]
        xpad[pl.ds(halo + entries, halo), :] = flip(hi_ref[...])[:halo]
        dots_ref[...] = jnp.zeros(dots_ref.shape, dots_ref.dtype)

        def turn(c, carry):
            col = pl.multiple_of(c * chunk, chunk)
            xpad[pl.ds(halo + col, chunk), :] = flip(xbuf[:, pl.ds(col, chunk)])
            return carry

        for p in range(pieces):
            copies[p].wait()
            lax.fori_loop(p * piece // chunk, (p + 1) * piece // chunk, turn, 0)

    def body(j, carry):
        row = g * group + j
        parts = []
        for k in range(NNZ):
            src = row + shift_ref[row * NNZ + k] + HALO
            start = pl.multiple_of(src * blk, 16)
            parts.append(xpad[pl.ds(start, blk), :])
        xs = jnp.concatenate(parts, axis=0)
        lhs = jnp.concatenate([m[j] for m in mats], axis=0) if nmat > 1 else mats[0][j]
        r = jnp.dot(lhs, xs, preferred_element_type=jnp.float32)
        for m in range(nmat):
            part = r[m * blk : (m + 1) * blk]
            accs[m][pl.ds(pl.multiple_of(j * blk, 16), blk), :] = part.astype(accs[m].dtype)
        return carry

    lax.fori_loop(0, group, body, 0, unroll=32)
    live = lax.broadcasted_iota(jnp.int32, (slots, chunk), 0) < count_ref[0]
    for c in range(span // chunk):
        if given:
            other = jnp.where(live, pair_ref[:, pl.ds(c * chunk, chunk)], jnp.zeros((), pair_ref.dtype))
        else:
            other = xbuf[:, pl.ds(pl.multiple_of(g * span + c * chunk, chunk), chunk)]
        for m in range(nmat):
            native = flip(accs[m][pl.ds(c * chunk, chunk), :])
            if keep:
                outs[m][:, pl.ds(c * chunk, chunk)] = native
            if given:
                dots_ref[m] += nt(native, other)
            else:
                dots_ref[m] += nt(other, native)


def block_apply(matrices, shifts_flat, count, cells, lower, upper, pair=None):
    slots, entries = cells.shape
    block_rows, blk, width = matrices[0].shape
    rim = lower.shape[1]
    group = 32 if block_rows % 32 == 0 else block_rows
    chunk = 512
    nmat = len(matrices)
    given = pair is not None
    keep = not given
    kernel = functools.partial(
        apply_kernel, group=group, blk=blk, nmat=nmat, chunk=chunk, keep=keep, given=given
    )
    mat_spec = pl.BlockSpec((group, blk, width), lambda g, s, n: (g, 0, 0))
    out_spec = pl.BlockSpec((slots, group * blk), lambda g, s, n: (0, g))
    halo_spec = pl.BlockSpec((slots, rim), lambda g, s, n: (0, 0))
    dots_spec = pl.BlockSpec((nmat, slots, slots), lambda g, s, n: (0, 0, 0))
    in_specs = [pl.BlockSpec(memory_space=pl.ANY), halo_spec, halo_spec] + [mat_spec] * nmat
    operands = [shifts_flat, count, cells, lower, upper, *matrices]
    if given:
        in_specs.append(out_spec)
        operands.append(pair)
    out_specs = ([out_spec] * nmat if keep else []) + [dots_spec]
    out_shape = ([jax.ShapeDtypeStruct((slots, entries), jnp.bfloat16)] * nmat if keep else []) + [
        jax.ShapeDtypeStruct((nmat, slots, slots), jnp.float32)
    ]
    grid_spec = pltpu.PrefetchScalarGridSpec(
        num_scalar_prefetch=2,
        grid=(block_rows // group,),
        in_specs=in_specs,
        out_specs=out_specs,
        scratch_shapes=[pltpu.VMEM((group * blk, slots), jnp.bfloat16)] * nmat
        + [
            pltpu.VMEM((slots, entries), cells.dtype),
            pltpu.VMEM((entries + 2 * HALO * blk, slots), cells.dtype),
            pltpu.SemaphoreType.DMA((4 if entries % (4 * chunk) == 0 else 1,)),
        ],
    )
    return pl.pallas_call(
        kernel,
        grid_spec=grid_spec,
        out_shape=out_shape,
        compiler_params=pltpu.CompilerParams(
            dimension_semantics=("arbitrary",), vmem_limit_bytes=56 * 1024 * 1024
        ),
    )(*operands)


def row_sum(part):
    count = lax.axis_size("row")
    here = lax.axis_index("row")
    got = [part] + [
        lax.ppermute(part, "row", [(i, (i + step) % count) for i in range(count)])
        for step in range(1, count)
    ]
    stacked = jnp.stack(got)
    total = None
    for source in range(count):
        term = lax.dynamic_index_in_dim(stacked, (here - source) % count, 0, keepdims=False)
        total = term if total is None else total + term
    return total


def shards(vectors, counts, offsets, margin_blocks, energy_blocks, block_columns):
    own_vectors = vectors[0]
    vector_count, entries = own_vectors.shape
    nmat_total = entries * lax.axis_size("row")
    block_rows = margin_blocks.shape[0]
    valid_mask = jnp.arange(vector_count, dtype=jnp.int32) < counts[0]
    window_rows = jnp.arange(WIN, dtype=jnp.int32)[:, None]
    lower_window = jnp.where(
        window_rows + offsets[0, 0] < counts[0],
        lax.dynamic_slice_in_dim(own_vectors, offsets[0, 0], WIN, 0),
        jnp.zeros((), own_vectors.dtype),
    )
    upper_window = jnp.where(
        window_rows + offsets[0, 1] < counts[0],
        lax.dynamic_slice_in_dim(own_vectors, offsets[0, 1], WIN, 0),
        jnp.zeros((), own_vectors.dtype),
    )
    own_blocks = lax.axis_index("row") * block_rows + jnp.arange(block_rows, dtype=jnp.int32)
    shifts_flat = (block_columns - own_blocks[:, None]).reshape(-1)
    cuts_count = lax.axis_size("cuts")
    odd = lax.axis_index("cuts") % 2 == 1
    evens = range(0, cuts_count, 2)
    odds = range(1, cuts_count, 2)
    rim = 256

    def exchange(upper, lower):
        return (
            from_behind(upper, "cuts", 1),
            from_behind(lower, "cuts", -1),
            lax.ppermute(upper, "cuts", [(i, i + 2) for i in evens if i + 2 < cuts_count]),
            lax.ppermute(lower, "cuts", [(i, i - 2) for i in odds if i - 2 >= 0]),
        )

    def finish(upper_1, lower_1, upper_direct, lower_direct):
        upper_2 = jnp.where(
            odd, lax.ppermute(upper_1, "cuts", [(i, i + 1) for i in evens if i + 1 < cuts_count]), upper_direct
        )
        lower_2 = jnp.where(odd, lower_direct, lax.ppermute(lower_1, "cuts", [(i, i - 1) for i in odds]))
        return [upper_2, upper_1, lower_1, lower_2]

    masked = jnp.where(valid_mask[:, None], own_vectors, jnp.zeros((), own_vectors.dtype))

    def edge_rows(start, cols):
        rows = lax.dynamic_slice_in_dim(own_vectors[:, cols], start, WIN, 0)
        return jnp.where(window_rows + start < counts[0], rows, jnp.zeros((), rows.dtype))

    def edges_of(cols):
        return jnp.concatenate(
            [edge_rows(offsets[0, 1], cols), edge_rows(offsets[0, 0], cols), masked[:, cols]], axis=0
        )

    below = lax.ppermute(
        edges_of(slice(entries - rim, entries)), "row", [(i, i + 1) for i in range(lax.axis_size("row") - 1)]
    )
    above = lax.ppermute(edges_of(slice(0, rim)), "row", [(i + 1, i) for i in range(lax.axis_size("row") - 1)])
    masked_lower, masked_upper = below[2 * WIN :], above[2 * WIN :]
    upper_ext = jnp.concatenate([upper_window, below[:WIN], above[:WIN]], axis=1)
    lower_ext = jnp.concatenate([lower_window, below[WIN : 2 * WIN], above[WIN : 2 * WIN]], axis=1)
    big = exchange(upper_ext, lower_ext)
    row_major = Layout(major_to_minor=(0, 1, 2))
    margin_blocks = with_layout_constraint(margin_blocks, row_major)
    energy_blocks = with_layout_constraint(energy_blocks, row_major)
    big, margin_blocks, energy_blocks = lax.optimization_barrier((big, margin_blocks, energy_blocks))
    received = jnp.concatenate(finish(*big), axis=0)
    windows = received[:, :entries]
    windows_lower = received[:, entries : entries + rim]
    windows_upper = received[:, entries + rim :]
    count = counts[:1]
    (margin_dots,) = block_apply(
        (margin_blocks,), shifts_flat, count, windows, windows_lower, windows_upper, pair=own_vectors
    )
    margin = row_sum(margin_dots[0]) / nmat_total
    margin_b = margin.astype(jnp.bfloat16)

    def clean(kept, wins):
        removed = lax.dot_general(margin_b, wins, (((0,), (0,)), ((), ())), preferred_element_type=jnp.float32)
        return (kept.astype(jnp.float32) - removed).astype(jnp.bfloat16)

    cleaned = clean(masked, windows)
    margin_cleaned, energy_cleaned, pencil_dots = block_apply(
        (margin_blocks, energy_blocks),
        shifts_flat,
        count,
        cleaned,
        clean(masked_lower, windows_lower),
        clean(masked_upper, windows_upper),
    )
    eye = jnp.arange(vector_count)[:, None] == jnp.arange(vector_count)[None, :]
    diagonals = row_sum(jnp.sum(jnp.where(eye[None], pencil_dots, 0.0), axis=2)) / nmat_total
    margin_diag = diagonals[0]
    energy_diag = diagonals[1]
    pencils = row_sum(pencil_dots) / nmat_total
    margin_pencil = pencils[0]
    energy_pencil = pencils[1]
    theta = jnp.where(
        valid_mask,
        energy_diag / jnp.where(valid_mask, margin_diag, jnp.float32(1.0)),
        jnp.float32(0.0),
    )
    residual = (
        energy_cleaned.astype(jnp.float32) - theta[:, None] * margin_cleaned.astype(jnp.float32)
    ).astype(jnp.bfloat16)
    return (residual[None], margin_pencil[None], energy_pencil[None])


def solution(mesh):
    placed = (
        P("cuts", None, "row"),
        P("cuts"),
        P("cuts", None),
        P("row", None, None),
        P("row", None, None),
        P("row", None),
    )
    return jax.shard_map(
        shards,
        mesh=mesh,
        in_specs=placed,
        out_specs=(P("cuts", None, "row"), P("cuts", None, None), P("cuts", None, None)),
        check_vma=False,
    )
```

```python
import functools

import jax
import jax.numpy as jnp
from jax import lax
from jax.experimental import pallas as pl
from jax.experimental.pallas import tpu as pltpu
from jax.experimental.layout import Layout, with_layout_constraint
from jax.sharding import PartitionSpec as P

WIN = 32
NNZ = 3
HALO = 2


def from_behind(block, axis, distance):
    devices = range(lax.axis_size(axis))
    route = [(i - distance, i) for i in devices if i - distance in devices]
    return lax.ppermute(block, axis, route)


def row_halos(cells, width):
    count = lax.axis_size("row")
    ends = count - 1
    head = cells[:, :width]
    tail = cells[:, cells.shape[1] - width :]
    lower = lax.ppermute(tail, "row", [(i, i + 1) for i in range(ends)])
    upper = lax.ppermute(head, "row", [(i + 1, i) for i in range(ends)])
    return lower, upper


def flip(tile):
    return tile.T


def nt(a, b):
    return lax.dot_general(a, b, (((1,), (1,)), ((), ())), preferred_element_type=jnp.float32)


def apply_kernel(shift_ref, count_ref, x_hbm, lo_ref, hi_ref, *refs, group, blk, nmat, chunk, keep, given):
    mats = refs[:nmat]
    at = nmat
    pair_ref = None
    if given:
        pair_ref = refs[at]
        at += 1
    outs = refs[at : at + nmat] if keep else ()
    at += nmat if keep else 0
    dots_ref = refs[at]
    accs = refs[at + 1 : at + 1 + nmat]
    xbuf, xpad, sem = refs[at + 1 + nmat :]
    g = pl.program_id(0)
    slots, entries = x_hbm.shape
    halo = HALO * blk
    rim = lo_ref.shape[1]
    span = group * blk

    @pl.when(g == 0)
    def _():
        pieces = sem.shape[0]
        piece = entries // pieces
        copies = [
            pltpu.make_async_copy(
                x_hbm.at[:, pl.ds(p * piece, piece)], xbuf.at[:, pl.ds(p * piece, piece)], sem.at[p]
            )
            for p in range(pieces)
        ]
        for copy in copies:
            copy.start()
        xpad[pl.ds(0, halo), :] = flip(lo_ref[...])[rim - halo :]
        xpad[pl.ds(halo + entries, halo), :] = flip(hi_ref[...])[:halo]
        dots_ref[...] = jnp.zeros(dots_ref.shape, dots_ref.dtype)

        def turn(c, carry):
            col = pl.multiple_of(c * chunk, chunk)
            xpad[pl.ds(halo + col, chunk), :] = flip(xbuf[:, pl.ds(col, chunk)])
            return carry

        for p in range(pieces):
            copies[p].wait()
            lax.fori_loop(p * piece // chunk, (p + 1) * piece // chunk, turn, 0)

    def body(j, carry):
        row = g * group + j
        parts = []
        for k in range(NNZ):
            src = row + shift_ref[row * NNZ + k] + HALO
            start = pl.multiple_of(src * blk, 16)
            parts.append(xpad[pl.ds(start, blk), :])
        xs = jnp.concatenate(parts, axis=0)
        lhs = jnp.concatenate([m[j] for m in mats], axis=0) if nmat > 1 else mats[0][j]
        r = jnp.dot(lhs, xs, preferred_element_type=jnp.float32)
        for m in range(nmat):
            part = r[m * blk : (m + 1) * blk]
            accs[m][pl.ds(pl.multiple_of(j * blk, 16), blk), :] = part.astype(accs[m].dtype)
        return carry

    lax.fori_loop(0, group, body, 0, unroll=16)
    live = lax.broadcasted_iota(jnp.int32, (slots, chunk), 0) < count_ref[0]
    for c in range(span // chunk):
        if given:
            other = jnp.where(live, pair_ref[:, pl.ds(c * chunk, chunk)], jnp.zeros((), pair_ref.dtype))
        else:
            other = xbuf[:, pl.ds(pl.multiple_of(g * span + c * chunk, chunk), chunk)]
        for m in range(nmat):
            native = flip(accs[m][pl.ds(c * chunk, chunk), :])
            if keep:
                outs[m][:, pl.ds(c * chunk, chunk)] = native
            if given:
                dots_ref[m] += nt(native, other)
            else:
                dots_ref[m] += nt(other, native)


def block_apply(matrices, shifts_flat, count, cells, lower, upper, pair=None):
    slots, entries = cells.shape
    block_rows, blk, width = matrices[0].shape
    rim = lower.shape[1]
    group = 16 if block_rows % 16 == 0 else block_rows
    chunk = 512
    nmat = len(matrices)
    given = pair is not None
    keep = not given
    kernel = functools.partial(
        apply_kernel, group=group, blk=blk, nmat=nmat, chunk=chunk, keep=keep, given=given
    )
    mat_spec = pl.BlockSpec((group, blk, width), lambda g, s, n: (g, 0, 0))
    out_spec = pl.BlockSpec((slots, group * blk), lambda g, s, n: (0, g))
    halo_spec = pl.BlockSpec((slots, rim), lambda g, s, n: (0, 0))
    dots_spec = pl.BlockSpec((nmat, slots, slots), lambda g, s, n: (0, 0, 0))
    in_specs = [pl.BlockSpec(memory_space=pl.ANY), halo_spec, halo_spec] + [mat_spec] * nmat
    operands = [shifts_flat, count, cells, lower, upper, *matrices]
    if given:
        in_specs.append(out_spec)
        operands.append(pair)
    out_specs = ([out_spec] * nmat if keep else []) + [dots_spec]
    out_shape = ([jax.ShapeDtypeStruct((slots, entries), jnp.bfloat16)] * nmat if keep else []) + [
        jax.ShapeDtypeStruct((nmat, slots, slots), jnp.float32)
    ]
    grid_spec = pltpu.PrefetchScalarGridSpec(
        num_scalar_prefetch=2,
        grid=(block_rows // group,),
        in_specs=in_specs,
        out_specs=out_specs,
        scratch_shapes=[pltpu.VMEM((group * blk, slots), jnp.bfloat16)] * nmat
        + [
            pltpu.VMEM((slots, entries), cells.dtype),
            pltpu.VMEM((entries + 2 * HALO * blk, slots), cells.dtype),
            pltpu.SemaphoreType.DMA((4 if entries % (4 * chunk) == 0 else 1,)),
        ],
    )
    return pl.pallas_call(
        kernel,
        grid_spec=grid_spec,
        out_shape=out_shape,
        compiler_params=pltpu.CompilerParams(
            dimension_semantics=("arbitrary",), vmem_limit_bytes=56 * 1024 * 1024
        ),
    )(*operands)


def row_sum(part):
    count = lax.axis_size("row")
    here = lax.axis_index("row")
    got = [part] + [
        lax.ppermute(part, "row", [(i, (i + step) % count) for i in range(count)])
        for step in range(1, count)
    ]
    stacked = jnp.stack(got)
    total = None
    for source in range(count):
        term = lax.dynamic_index_in_dim(stacked, (here - source) % count, 0, keepdims=False)
        total = term if total is None else total + term
    return total


def shards(vectors, counts, offsets, margin_blocks, energy_blocks, block_columns):
    own_vectors = vectors[0]
    vector_count, entries = own_vectors.shape
    nmat_total = entries * lax.axis_size("row")
    block_rows = margin_blocks.shape[0]
    valid_mask = jnp.arange(vector_count, dtype=jnp.int32) < counts[0]
    window_rows = jnp.arange(WIN, dtype=jnp.int32)[:, None]
    lower_window = jnp.where(
        window_rows + offsets[0, 0] < counts[0],
        lax.dynamic_slice_in_dim(own_vectors, offsets[0, 0], WIN, 0),
        jnp.zeros((), own_vectors.dtype),
    )
    upper_window = jnp.where(
        window_rows + offsets[0, 1] < counts[0],
        lax.dynamic_slice_in_dim(own_vectors, offsets[0, 1], WIN, 0),
        jnp.zeros((), own_vectors.dtype),
    )
    own_blocks = lax.axis_index("row") * block_rows + jnp.arange(block_rows, dtype=jnp.int32)
    shifts_flat = (block_columns - own_blocks[:, None]).reshape(-1)
    cuts_count = lax.axis_size("cuts")
    odd = lax.axis_index("cuts") % 2 == 1
    evens = range(0, cuts_count, 2)
    odds = range(1, cuts_count, 2)
    rim = 256

    def exchange(upper, lower):
        return (
            from_behind(upper, "cuts", 1),
            from_behind(lower, "cuts", -1),
            lax.ppermute(upper, "cuts", [(i, i + 2) for i in evens if i + 2 < cuts_count]),
            lax.ppermute(lower, "cuts", [(i, i - 2) for i in odds if i - 2 >= 0]),
        )

    def finish(upper_1, lower_1, upper_direct, lower_direct):
        upper_2 = jnp.where(
            odd, lax.ppermute(upper_1, "cuts", [(i, i + 1) for i in evens if i + 1 < cuts_count]), upper_direct
        )
        lower_2 = jnp.where(odd, lower_direct, lax.ppermute(lower_1, "cuts", [(i, i - 1) for i in odds]))
        return [upper_2, upper_1, lower_1, lower_2]

    masked = jnp.where(valid_mask[:, None], own_vectors, jnp.zeros((), own_vectors.dtype))

    def edge_rows(start, cols):
        rows = lax.dynamic_slice_in_dim(own_vectors[:, cols], start, WIN, 0)
        return jnp.where(window_rows + start < counts[0], rows, jnp.zeros((), rows.dtype))

    def edges_of(cols):
        return jnp.concatenate(
            [edge_rows(offsets[0, 1], cols), edge_rows(offsets[0, 0], cols), masked[:, cols]], axis=0
        )

    below = lax.ppermute(
        edges_of(slice(entries - rim, entries)), "row", [(i, i + 1) for i in range(lax.axis_size("row") - 1)]
    )
    above = lax.ppermute(edges_of(slice(0, rim)), "row", [(i + 1, i) for i in range(lax.axis_size("row") - 1)])
    masked_lower, masked_upper = below[2 * WIN :], above[2 * WIN :]
    upper_ext = jnp.concatenate([upper_window, below[:WIN], above[:WIN]], axis=1)
    lower_ext = jnp.concatenate([lower_window, below[WIN : 2 * WIN], above[WIN : 2 * WIN]], axis=1)
    big = exchange(upper_ext, lower_ext)
    row_major = Layout(major_to_minor=(0, 1, 2))
    margin_blocks = with_layout_constraint(margin_blocks, row_major)
    energy_blocks = with_layout_constraint(energy_blocks, row_major)
    big, margin_blocks, energy_blocks = lax.optimization_barrier((big, margin_blocks, energy_blocks))
    received = jnp.concatenate(finish(*big), axis=0)
    windows = received[:, :entries]
    windows_lower = received[:, entries : entries + rim]
    windows_upper = received[:, entries + rim :]
    count = counts[:1]
    (margin_dots,) = block_apply(
        (margin_blocks,), shifts_flat, count, windows, windows_lower, windows_upper, pair=own_vectors
    )
    margin = row_sum(margin_dots[0]) / nmat_total
    margin_b = margin.astype(jnp.bfloat16)

    def clean(kept, wins):
        removed = lax.dot_general(margin_b, wins, (((0,), (0,)), ((), ())), preferred_element_type=jnp.float32)
        return (kept.astype(jnp.float32) - removed).astype(jnp.bfloat16)

    cleaned = clean(masked, windows)
    margin_cleaned, energy_cleaned, pencil_dots = block_apply(
        (margin_blocks, energy_blocks),
        shifts_flat,
        count,
        cleaned,
        clean(masked_lower, windows_lower),
        clean(masked_upper, windows_upper),
    )
    eye = jnp.arange(vector_count)[:, None] == jnp.arange(vector_count)[None, :]
    diagonals = row_sum(jnp.sum(jnp.where(eye[None], pencil_dots, 0.0), axis=2)) / nmat_total
    margin_diag = diagonals[0]
    energy_diag = diagonals[1]
    pencils = row_sum(pencil_dots) / nmat_total
    margin_pencil = pencils[0]
    energy_pencil = pencils[1]
    theta = jnp.where(
        valid_mask,
        energy_diag / jnp.where(valid_mask, margin_diag, jnp.float32(1.0)),
        jnp.float32(0.0),
    )
    residual = (
        energy_cleaned.astype(jnp.float32) - theta[:, None] * margin_cleaned.astype(jnp.float32)
    ).astype(jnp.bfloat16)
    return (residual[None], margin_pencil[None], energy_pencil[None])


def solution(mesh):
    placed = (
        P("cuts", None, "row"),
        P("cuts"),
        P("cuts", None),
        P("row", None, None),
        P("row", None, None),
        P("row", None),
    )
    return jax.shard_map(
        shards,
        mesh=mesh,
        in_specs=placed,
        out_specs=(P("cuts", None, "row"), P("cuts", None, None), P("cuts", None, None)),
        check_vma=False,
    )
```

```python
import functools

import jax
import jax.numpy as jnp
from jax import lax
from jax.experimental import pallas as pl
from jax.experimental.pallas import tpu as pltpu
from jax.experimental.layout import Layout, with_layout_constraint
from jax.sharding import PartitionSpec as P

WIN = 32
NNZ = 3
HALO = 2


def from_behind(block, axis, distance):
    devices = range(lax.axis_size(axis))
    route = [(i - distance, i) for i in devices if i - distance in devices]
    return lax.ppermute(block, axis, route)


def row_halos(cells, width):
    count = lax.axis_size("row")
    ends = count - 1
    head = cells[:, :width]
    tail = cells[:, cells.shape[1] - width :]
    lower = lax.ppermute(tail, "row", [(i, i + 1) for i in range(ends)])
    upper = lax.ppermute(head, "row", [(i + 1, i) for i in range(ends)])
    return lower, upper


def flip(tile):
    return tile.T


def nt(a, b):
    return lax.dot_general(a, b, (((1,), (1,)), ((), ())), preferred_element_type=jnp.float32)


def apply_kernel(shift_ref, count_ref, x_hbm, lo_ref, hi_ref, *refs, group, blk, nmat, chunk, keep, given):
    mats = refs[:nmat]
    at = nmat
    pair_ref = None
    if given:
        pair_ref = refs[at]
        at += 1
    outs = refs[at : at + nmat] if keep else ()
    at += nmat if keep else 0
    dots_ref = refs[at]
    accs = refs[at + 1 : at + 1 + nmat]
    xbuf, xpad, sem = refs[at + 1 + nmat :]
    g = pl.program_id(0)
    slots, entries = x_hbm.shape
    halo = HALO * blk
    rim = lo_ref.shape[1]
    span = group * blk

    @pl.when(g == 0)
    def _():
        pieces = sem.shape[0]
        piece = entries // pieces
        copies = [
            pltpu.make_async_copy(
                x_hbm.at[:, pl.ds(p * piece, piece)], xbuf.at[:, pl.ds(p * piece, piece)], sem.at[p]
            )
            for p in range(pieces)
        ]
        for copy in copies:
            copy.start()
        xpad[pl.ds(0, halo), :] = flip(lo_ref[...])[rim - halo :]
        xpad[pl.ds(halo + entries, halo), :] = flip(hi_ref[...])[:halo]
        dots_ref[...] = jnp.zeros(dots_ref.shape, dots_ref.dtype)

        def turn(c, carry):
            col = pl.multiple_of(c * chunk, chunk)
            xpad[pl.ds(halo + col, chunk), :] = flip(xbuf[:, pl.ds(col, chunk)])
            return carry

        for p in range(pieces):
            copies[p].wait()
            lax.fori_loop(p * piece // chunk, (p + 1) * piece // chunk, turn, 0)

    def body(j, carry):
        row = g * group + j
        parts = []
        for k in range(NNZ):
            src = row + shift_ref[row * NNZ + k] + HALO
            start = pl.multiple_of(src * blk, 16)
            parts.append(xpad[pl.ds(start, blk), :])
        xs = jnp.concatenate(parts, axis=0)
        lhs = jnp.concatenate([m[j] for m in mats], axis=0) if nmat > 1 else mats[0][j]
        r = jnp.dot(lhs, xs, preferred_element_type=jnp.float32)
        for m in range(nmat):
            part = r[m * blk : (m + 1) * blk]
            accs[m][pl.ds(pl.multiple_of(j * blk, 16), blk), :] = part.astype(accs[m].dtype)
        return carry

    lax.fori_loop(0, group, body, 0, unroll=32)
    live = lax.broadcasted_iota(jnp.int32, (slots, chunk), 0) < count_ref[0]
    for c in range(span // chunk):
        if given:
            other = jnp.where(live, pair_ref[:, pl.ds(c * chunk, chunk)], jnp.zeros((), pair_ref.dtype))
        else:
            other = xbuf[:, pl.ds(pl.multiple_of(g * span + c * chunk, chunk), chunk)]
        for m in range(nmat):
            native = flip(accs[m][pl.ds(c * chunk, chunk), :])
            if keep:
                outs[m][:, pl.ds(c * chunk, chunk)] = native
            if given:
                dots_ref[m] += nt(native, other)
            else:
                dots_ref[m] += nt(other, native)


def block_apply(matrices, shifts_flat, count, cells, lower, upper, pair=None):
    slots, entries = cells.shape
    block_rows, blk, width = matrices[0].shape
    rim = lower.shape[1]
    group = 32 if block_rows % 32 == 0 else block_rows
    chunk = 1024
    nmat = len(matrices)
    given = pair is not None
    keep = not given
    kernel = functools.partial(
        apply_kernel, group=group, blk=blk, nmat=nmat, chunk=chunk, keep=keep, given=given
    )
    mat_spec = pl.BlockSpec((group, blk, width), lambda g, s, n: (g, 0, 0))
    out_spec = pl.BlockSpec((slots, group * blk), lambda g, s, n: (0, g))
    halo_spec = pl.BlockSpec((slots, rim), lambda g, s, n: (0, 0))
    dots_spec = pl.BlockSpec((nmat, slots, slots), lambda g, s, n: (0, 0, 0))
    in_specs = [pl.BlockSpec(memory_space=pl.ANY), halo_spec, halo_spec] + [mat_spec] * nmat
    operands = [shifts_flat, count, cells, lower, upper, *matrices]
    if given:
        in_specs.append(out_spec)
        operands.append(pair)
    out_specs = ([out_spec] * nmat if keep else []) + [dots_spec]
    out_shape = ([jax.ShapeDtypeStruct((slots, entries), jnp.bfloat16)] * nmat if keep else []) + [
        jax.ShapeDtypeStruct((nmat, slots, slots), jnp.float32)
    ]
    grid_spec = pltpu.PrefetchScalarGridSpec(
        num_scalar_prefetch=2,
        grid=(block_rows // group,),
        in_specs=in_specs,
        out_specs=out_specs,
        scratch_shapes=[pltpu.VMEM((group * blk, slots), jnp.bfloat16)] * nmat
        + [
            pltpu.VMEM((slots, entries), cells.dtype),
            pltpu.VMEM((entries + 2 * HALO * blk, slots), cells.dtype),
            pltpu.SemaphoreType.DMA((4 if entries % (4 * chunk) == 0 else 1,)),
        ],
    )
    return pl.pallas_call(
        kernel,
        grid_spec=grid_spec,
        out_shape=out_shape,
        compiler_params=pltpu.CompilerParams(
            dimension_semantics=("arbitrary",), vmem_limit_bytes=56 * 1024 * 1024
        ),
    )(*operands)


def row_sum(part):
    count = lax.axis_size("row")
    here = lax.axis_index("row")
    got = [part] + [
        lax.ppermute(part, "row", [(i, (i + step) % count) for i in range(count)])
        for step in range(1, count)
    ]
    stacked = jnp.stack(got)
    total = None
    for source in range(count):
        term = lax.dynamic_index_in_dim(stacked, (here - source) % count, 0, keepdims=False)
        total = term if total is None else total + term
    return total


def shards(vectors, counts, offsets, margin_blocks, energy_blocks, block_columns):
    own_vectors = vectors[0]
    vector_count, entries = own_vectors.shape
    nmat_total = entries * lax.axis_size("row")
    block_rows = margin_blocks.shape[0]
    valid_mask = jnp.arange(vector_count, dtype=jnp.int32) < counts[0]
    window_rows = jnp.arange(WIN, dtype=jnp.int32)[:, None]
    lower_window = jnp.where(
        window_rows + offsets[0, 0] < counts[0],
        lax.dynamic_slice_in_dim(own_vectors, offsets[0, 0], WIN, 0),
        jnp.zeros((), own_vectors.dtype),
    )
    upper_window = jnp.where(
        window_rows + offsets[0, 1] < counts[0],
        lax.dynamic_slice_in_dim(own_vectors, offsets[0, 1], WIN, 0),
        jnp.zeros((), own_vectors.dtype),
    )
    own_blocks = lax.axis_index("row") * block_rows + jnp.arange(block_rows, dtype=jnp.int32)
    shifts_flat = (block_columns - own_blocks[:, None]).reshape(-1)
    cuts_count = lax.axis_size("cuts")
    odd = lax.axis_index("cuts") % 2 == 1
    evens = range(0, cuts_count, 2)
    odds = range(1, cuts_count, 2)
    rim = 256

    def exchange(upper, lower):
        return (
            from_behind(upper, "cuts", 1),
            from_behind(lower, "cuts", -1),
            lax.ppermute(upper, "cuts", [(i, i + 2) for i in evens if i + 2 < cuts_count]),
            lax.ppermute(lower, "cuts", [(i, i - 2) for i in odds if i - 2 >= 0]),
        )

    def finish(upper_1, lower_1, upper_direct, lower_direct):
        upper_2 = jnp.where(
            odd, lax.ppermute(upper_1, "cuts", [(i, i + 1) for i in evens if i + 1 < cuts_count]), upper_direct
        )
        lower_2 = jnp.where(odd, lower_direct, lax.ppermute(lower_1, "cuts", [(i, i - 1) for i in odds]))
        return [upper_2, upper_1, lower_1, lower_2]

    masked = jnp.where(valid_mask[:, None], own_vectors, jnp.zeros((), own_vectors.dtype))

    def edge_rows(start, cols):
        rows = lax.dynamic_slice_in_dim(own_vectors[:, cols], start, WIN, 0)
        return jnp.where(window_rows + start < counts[0], rows, jnp.zeros((), rows.dtype))

    def edges_of(cols):
        return jnp.concatenate(
            [edge_rows(offsets[0, 1], cols), edge_rows(offsets[0, 0], cols), masked[:, cols]], axis=0
        )

    below = lax.ppermute(
        edges_of(slice(entries - rim, entries)), "row", [(i, i + 1) for i in range(lax.axis_size("row") - 1)]
    )
    above = lax.ppermute(edges_of(slice(0, rim)), "row", [(i + 1, i) for i in range(lax.axis_size("row") - 1)])
    masked_lower, masked_upper = below[2 * WIN :], above[2 * WIN :]
    upper_ext = jnp.concatenate([upper_window, below[:WIN], above[:WIN]], axis=1)
    lower_ext = jnp.concatenate([lower_window, below[WIN : 2 * WIN], above[WIN : 2 * WIN]], axis=1)
    big = exchange(upper_ext, lower_ext)
    row_major = Layout(major_to_minor=(0, 1, 2))
    margin_blocks = with_layout_constraint(margin_blocks, row_major)
    energy_blocks = with_layout_constraint(energy_blocks, row_major)
    big, margin_blocks, energy_blocks = lax.optimization_barrier((big, margin_blocks, energy_blocks))
    received = jnp.concatenate(finish(*big), axis=0)
    windows = received[:, :entries]
    windows_lower = received[:, entries : entries + rim]
    windows_upper = received[:, entries + rim :]
    count = counts[:1]
    (margin_dots,) = block_apply(
        (margin_blocks,), shifts_flat, count, windows, windows_lower, windows_upper, pair=own_vectors
    )
    margin = row_sum(margin_dots[0]) / nmat_total
    margin_b = margin.astype(jnp.bfloat16)

    def clean(kept, wins):
        removed = lax.dot_general(margin_b, wins, (((0,), (0,)), ((), ())), preferred_element_type=jnp.float32)
        return (kept.astype(jnp.float32) - removed).astype(jnp.bfloat16)

    cleaned = clean(masked, windows)
    margin_cleaned, energy_cleaned, pencil_dots = block_apply(
        (margin_blocks, energy_blocks),
        shifts_flat,
        count,
        cleaned,
        clean(masked_lower, windows_lower),
        clean(masked_upper, windows_upper),
    )
    eye = jnp.arange(vector_count)[:, None] == jnp.arange(vector_count)[None, :]
    diagonals = row_sum(jnp.sum(jnp.where(eye[None], pencil_dots, 0.0), axis=2)) / nmat_total
    margin_diag = diagonals[0]
    energy_diag = diagonals[1]
    pencils = row_sum(pencil_dots) / nmat_total
    margin_pencil = pencils[0]
    energy_pencil = pencils[1]
    theta = jnp.where(
        valid_mask,
        energy_diag / jnp.where(valid_mask, margin_diag, jnp.float32(1.0)),
        jnp.float32(0.0),
    )
    residual = (
        energy_cleaned.astype(jnp.float32) - theta[:, None] * margin_cleaned.astype(jnp.float32)
    ).astype(jnp.bfloat16)
    return (residual[None], margin_pencil[None], energy_pencil[None])


def solution(mesh):
    placed = (
        P("cuts", None, "row"),
        P("cuts"),
        P("cuts", None),
        P("row", None, None),
        P("row", None, None),
        P("row", None),
    )
    return jax.shard_map(
        shards,
        mesh=mesh,
        in_specs=placed,
        out_specs=(P("cuts", None, "row"), P("cuts", None, None), P("cuts", None, None)),
        check_vma=False,
    )
```
